512 devices in a mesh: context: 64 (over x, z), tensor: 8 (over y, core).
Axes of the slice: x: 4, y: 4, z: 16, core: 2. Of those that a mesh axis runs over, the one named last changes fastest.
Arguments:
- inputs: bfloat16 [8192, 8192], P('context', 'tensor'), may hold values from -0.8984375 to 0.8984375
- grads: bfloat16 [8192, 8192], P('context', 'tensor'), may hold values from -0.8984375 to 0.8984375
- step_size: float32 [128, 8192], P('tensor', 'context'), may hold values from 0.25 to 4
- decay_rate: float32 [128], P('tensor'), may hold values from 0 to 1, as said below
- skip_gain: float32 [128], P('tensor'), may hold values from 0.5 to 1.5
- b_rows: bfloat16 [8192, 128], P(('context', 'tensor')), may hold values from -0.59765625 to 0.59765625
- c_rows: bfloat16 [8192, 128], P(('context', 'tensor')), may hold values from -0.59765625 to 0.59765625
- doc_lengths: int32 [64], replicated, may hold values from 1 to 1536, 8192 in all
Outputs:
- grad_x: float32 [8192, 8192], P('context', 'tensor')
- grad_step: float32 [128, 8192], P('tensor', 'context')
- grad_b: float32 [8192, 128], P(('context', 'tensor'))
- grad_c: float32 [8192, 128], P(('context', 'tensor'))
The draws below stay inside these ranges and needn't reach their ends.
Inputs may be any that keep to these rules, and one draw needn't show every extreme that they name: doc_lengths sum to 8192; the longest document has exactly 1536 tokens. `decay_rate`: decay rates are positive.
All inputs are finite; a program needn't handle non-finite values.
Results may differ from the reference program's by a relative error of at most 0.0005.
Values may be sent and summed in bfloat16 or wider, within the bound.
No kernel may reach another device: no remote copies, remote signals or barrier semaphores. Data moves between devices by JAX's collectives and lax.ppermute only.
A program may use at most 192 MiB of HBM per device.

```python
import math
import jax
import jax.numpy as jnp
import numpy as np
from jax import lax

H = 128
P_SIZE = 64
N = 128
TOK_DEV = 128
TOKENS = 8192
DOCS = 64
DOC_MOST = 1536


def draw_decay_rate(key, part):
    key_pick, key_fast, key_slow = jax.random.split(jax.random.fold_in(key, 11), 3)
    fast = jax.random.uniform(key_pick, (H,)) < 0.5
    fast_rate = jnp.exp(jax.random.uniform(key_fast, (H,), jnp.float32, jnp.log(1.0 / 40.0), jnp.log(1.0 / 20.0)))
    slow_rate = jnp.exp(jax.random.uniform(key_slow, (H,), jnp.float32, jnp.log(0.15), 0.0)) / DOC_MOST
    return jnp.where(fast, fast_rate, slow_rate).astype(jnp.float32)


def shard_levels(stream_key, extent, cuts, least, largest):
    def one(dim, blocks):
        steps = jax.random.uniform(jax.random.fold_in(jax.random.fold_in(stream_key, 6), dim), (blocks,), jnp.float32, least / len(cuts), largest / len(cuts))
        return jnp.repeat(jnp.exp(steps), extent[dim] // blocks).reshape((-1,) + (1,) * (len(extent) - dim - 1))

    level = one(*cuts[0])
    for cut in cuts[1:]:
        level = level * one(*cut)
    return level


def length_profile(count, total, limit, skew):
    weights = [(1 << 20) // math.isqrt(standing ** skew) + 1 for standing in range(2, count + 1)]
    rest, holding = total - limit - (count - 1), [1] * (count - 1)
    while rest > 0:
        candidates = [i for i in range(count - 1) if holding[i] < limit]
        pool, budget = sum([weights[i] for i in candidates]), rest
        for i in candidates:
            extra = min(limit - holding[i], max(1, budget * weights[i] // pool), rest)
            holding[i] = holding[i] + extra
            rest = rest - extra
    return np.array([limit] + holding)


def uneven_parts(rng, amount, total, most, skew):
    if amount == 2:
        one = jax.random.randint(rng, (), max(1, total - most), min(most, total - 1) + 1)
        return jnp.stack([one, total - one])
    tallies = jnp.asarray(length_profile(amount, total, most, skew), jnp.int32)
    couples = (amount - 1) // 2
    giver, receiver = tallies[1:1 + 2 * couples:2], tallies[2:2 + 2 * couples:2]
    room = jnp.minimum(giver - 1, most - receiver)
    shifted = jax.random.randint(jax.random.fold_in(rng, 1), (couples,), 0, 1 << 20) % (room + 1)
    tallies = tallies.at[1:1 + 2 * couples:2].set(giver - shifted).at[2:2 + 2 * couples:2].set(receiver + shifted)
    return tallies[jax.random.permutation(jax.random.fold_in(rng, 2), amount)]


def noise(key, shape, width, bound, cuts=(), held_as=jnp.bfloat16):
    level = shard_levels(key, shape, cuts, -0.22, 0.18) if cuts else 1.0
    entries = jax.random.normal(key, shape, jnp.float32) * width * level
    return jnp.minimum(jnp.maximum(entries, -bound), bound).astype(held_as)


def setup_inputs(seed: int = 0) -> dict:
    streams_of = jax.random.split(jax.random.key(seed), 9)
    return {
        "inputs": noise(streams_of[0], (TOKENS, H * P_SIZE), 0.15, 0.8984375, ((0, 64), (1, 8))),
        "grads": noise(streams_of[1], (TOKENS, H * P_SIZE), 0.15, 0.8984375, ((0, 64), (1, 8))),
        "step_size": jnp.clip(jnp.exp(math.log(4.0) - 2.7725887 * jax.random.uniform(streams_of[2], (H, TOKENS), jnp.float32) ** shard_levels(streams_of[2], (H, TOKENS), ((0, 8), (1, 64)), -0.2, 0.2)), 0.25, 4.0),
        "decay_rate": draw_decay_rate(jax.random.fold_in(streams_of[8], 71), 0),
        "skip_gain": jnp.clip(0.5 + 1.0 * jax.random.uniform(streams_of[4], (H,), jnp.float32) ** shard_levels(streams_of[4], (H,), ((0, 8),), -0.2, 0.2), 0.5, 1.5),
        "b_rows": noise(streams_of[5], (TOKENS, N), 0.1, 0.59765625, ((0, 512),)),
        "c_rows": noise(streams_of[6], (TOKENS, N), 0.1, 0.59765625, ((0, 512),)),
        "doc_lengths": uneven_parts(streams_of[7], DOCS, TOKENS, DOC_MOST, 2).astype(jnp.int32),
    }


HIGH = lax.Precision.HIGHEST

def block_pass(state, block, rate, skip):
    xb, dtb, bb, cb, segb = block
    logc = jnp.cumsum(-dtb * rate)
    index = jnp.arange(xb.shape[0])
    keep = (index[:, None] >= index[None, :]) & (segb[:, None] == segb[None, :])
    weights = jnp.exp(jnp.where(keep, logc[:, None] - logc[None, :], -1e+30))
    enter = jnp.exp(logc) * (segb == 0).astype(logc.dtype)
    moved = dtb[:, None] * xb
    scores = jnp.dot(cb, bb.T, precision=HIGH)
    out = jnp.dot(weights * scores, moved, precision=HIGH)
    out = out + enter[:, None] * jnp.dot(cb, state.T, precision=HIGH) + skip * xb
    new_state = jnp.dot((weights[-1][:, None] * moved).T, bb, precision=HIGH) + enter[-1] * state
    return (new_state, out)

def head_forward(xh, dth, bmat, cmat, rate, skip, seg):
    blocks = TOKENS // TOK_DEV
    data = (xh.reshape(blocks, TOK_DEV, P_SIZE), dth.reshape(blocks, TOK_DEV), bmat.reshape(blocks, TOK_DEV, N), cmat.reshape(blocks, TOK_DEV, N), seg.reshape(blocks, TOK_DEV))
    start = jnp.zeros((P_SIZE, N), xh.dtype)
    _, outs = lax.scan(lambda s, blk: block_pass(s, blk, rate, skip), start, data)
    return outs.reshape(TOKENS, P_SIZE)

def reference(inputs, grads, step_size, decay_rate, skip_gain, b_rows, c_rows, doc_lengths):
    blocks = TOKENS // TOK_DEV
    ends = jnp.cumsum(doc_lengths).astype(jnp.int32)
    starts = (ends - doc_lengths).astype(jnp.int32)
    is_start = jnp.zeros((TOKENS,), jnp.int32).at[starts].set(1)
    seg = jnp.cumsum(is_start.reshape(blocks, TOK_DEV), axis=1).reshape(TOKENS).astype(jnp.int32)
    bmat = b_rows.astype(jnp.float32)
    cmat = c_rows.astype(jnp.float32)

    def per_head(carry, head):
        xh = lax.dynamic_slice_in_dim(inputs, head * P_SIZE, P_SIZE, 1).astype(jnp.float32)
        dyh = lax.dynamic_slice_in_dim(grads, head * P_SIZE, P_SIZE, 1).astype(jnp.float32)
        dth = step_size[head]
        rate = decay_rate[head]
        skip = skip_gain[head]

        def forward(a, b, c, d):
            return head_forward(a, b, c, d, rate, skip, seg)
        _, pull = jax.vjp(forward, xh, dth, bmat, cmat)
        gx, gdt, gb, gc = pull(dyh)
        return ((carry[0] + gb, carry[1] + gc), (gx, gdt))
    zero = jnp.zeros((TOKENS, N), jnp.float32)
    (grad_b, grad_c), (gx, grad_step) = lax.scan(per_head, (zero, zero), jnp.arange(H, dtype=jnp.int32))
    grad_x = gx.transpose(1, 0, 2).reshape(TOKENS, H * P_SIZE)
    return (grad_x, grad_step, grad_b, grad_c)
```

```python
import jax
import jax.numpy as jnp
from jax import lax
from jax.sharding import PartitionSpec as P

HIGH = lax.Precision.HIGHEST


def from_behind(x, axis, by):
    peers = lax.axis_size(axis)
    pairs = [(i, i + by) for i in range(peers) if 0 <= i + by < peers]
    return lax.ppermute(x, axis, pairs)


def local(inputs, grads, step_size, decay_rate, skip_gain, b_rows, c_rows, doc_lengths):
    length = inputs.shape[0]
    heads = step_size.shape[0]
    width = inputs.shape[1] // heads
    rows = lax.all_gather(jnp.stack([b_rows, c_rows]), "tensor", axis=1, tiled=True)
    b_bf, c_bf = rows[0], rows[1]
    bmat = b_bf.astype(jnp.float32)
    cmat = c_bf.astype(jnp.float32)
    xs = inputs.astype(jnp.float32).reshape(length, heads, width).transpose(1, 0, 2)
    dys = grads.astype(jnp.float32).reshape(length, heads, width).transpose(1, 0, 2)
    offset = lax.axis_index("context") * length
    ends = jnp.cumsum(doc_lengths)
    starts = ends - doc_lengths
    position = offset + jnp.arange(length, dtype=jnp.int32)
    seg = jnp.sum(
        ((starts[None, :] >= offset) & (starts[None, :] <= position[:, None])).astype(jnp.int32),
        axis=1,
    )
    rate = decay_rate[:, None]
    logc = jnp.cumsum(-step_size * rate, axis=1)
    enter = jnp.exp(logc) * (seg == 0).astype(jnp.float32)[None, :]
    leave = jnp.exp(logc[:, -1:] - logc) * (seg == seg[-1]).astype(jnp.float32)[None, :]
    total = enter[:, -1][:, None, None]
    moved = step_size[:, :, None] * xs
    left_u = leave[:, :, None] * moved
    enter_dy = enter[:, :, None] * dys
    local_state = jnp.einsum("hlp,ln->hpn", left_u, bmat, precision=HIGH)
    local_adj = jnp.einsum("hlp,ln->hpn", enter_dy, cmat, precision=HIGH)

    turns = 3 * lax.axis_size("context") // 16
    inc_state = jnp.zeros_like(local_state)
    inc_adj = jnp.zeros_like(local_adj)
    for _ in range(turns):
        send_state, send_adj = lax.optimization_barrier(
            (local_state + total * inc_state, local_adj + total * inc_adj)
        )
        inc_state, inc_adj = lax.optimization_barrier(
            (from_behind(send_state, "context", 1), from_behind(send_adj, "context", -1))
        )
    s_in, g_in = inc_state, inc_adj

    index = jnp.arange(length)
    keep = (index[:, None] >= index[None, :]) & (seg[:, None] == seg[None, :])
    weights = jnp.exp(jnp.where(keep[None], logc[:, :, None] - logc[:, None, :], -1e30))
    scores = jnp.dot(c_bf, b_bf.T, preferred_element_type=jnp.float32)
    mixed = weights * scores[None]
    core_loc = jnp.einsum("hij,hip->hjp", mixed, dys, precision=HIGH)
    pairs = jnp.einsum("hip,hjp->hij", dys, moved, precision=HIGH)
    paired = mixed * pairs
    col_total = jnp.sum(paired, axis=1)
    row_total = jnp.sum(paired, axis=2)
    inner = jnp.cumsum(col_total, axis=1) - (jnp.cumsum(row_total, axis=1) - row_total)
    weighted = jnp.sum(weights * pairs, axis=0)
    gb_loc = jnp.dot(weighted.T, cmat, precision=HIGH)
    gc_loc = jnp.dot(weighted, bmat, precision=HIGH)

    b_adj = jnp.einsum("ln,hpn->hlp", bmat, g_in, precision=HIGH)
    c_state = jnp.einsum("ln,hpn->hlp", cmat, s_in, precision=HIGH)
    core = core_loc + leave[:, :, None] * b_adj
    gx = step_size[:, :, None] * core + skip_gain[:, None, None] * dys
    along = jnp.sum(xs * core, axis=2)
    from_state = enter * jnp.einsum(
        "hij,hi->hj", weights, jnp.sum(dys * c_state, axis=2), precision=HIGH
    )
    from_adj = leave * jnp.einsum(
        "hij,hj->hi", weights, jnp.sum(moved * b_adj, axis=2), precision=HIGH
    )
    both = leave * enter * jnp.sum(g_in * s_in, axis=(1, 2))[:, None]
    grad_step = along * (1.0 + rate * step_size) - rate * (inner + from_state + from_adj + both)
    gb = gb_loc + jnp.einsum("hlp,hpn->ln", left_u, g_in, precision=HIGH)
    gc = gc_loc + jnp.einsum("hlp,hpn->ln", enter_dy, s_in, precision=HIGH)

    grad_x = gx.transpose(1, 0, 2).reshape(length, heads * width)
    grad_bc = lax.psum_scatter(jnp.stack([gb, gc]), "tensor", scatter_dimension=1, tiled=True)
    return (grad_x, grad_step, grad_bc[0], grad_bc[1])


def solution(mesh):
    in_specs = (
        P("context", "tensor"),
        P("context", "tensor"),
        P("tensor", "context"),
        P("tensor"),
        P("tensor"),
        P(("context", "tensor"), None),
        P(("context", "tensor"), None),
        P(),
    )
    out_specs = (
        P("context", "tensor"),
        P("tensor", "context"),
        P(("context", "tensor"), None),
        P(("context", "tensor"), None),
    )
    return jax.shard_map(local, mesh=mesh, in_specs=in_specs, out_specs=out_specs, check_vma=False)
```

```python
import jax
import jax.numpy as jnp
from jax import lax
from jax.sharding import PartitionSpec as P

HIGH = lax.Precision.HIGHEST


def from_behind(x, axis, by):
    peers = lax.axis_size(axis)
    pairs = [(i, i + by) for i in range(peers) if 0 <= i + by < peers]
    return lax.ppermute(x, axis, pairs)


def shift_pair(fwd, bwd, by):
    fwd, bwd = lax.optimization_barrier((fwd, bwd))
    return lax.optimization_barrier(
        (from_behind(fwd, "context", by), from_behind(bwd, "context", -by))
    )


def exchange(pieces, axis):
    count = lax.axis_size(axis)
    pieces = lax.optimization_barrier(pieces)
    got = [
        lax.ppermute(pieces[s], axis, [(i, (i + s) % count) for i in range(count)])
        for s in range(1, count)
    ]
    return [pieces[0]] + list(lax.optimization_barrier(got))


def gather_rows(piece, axis):
    count = lax.axis_size(axis)
    me = lax.axis_index(axis)
    got = jnp.stack(exchange([piece] * count, axis))
    order = (me - jnp.arange(count)) % count
    return jnp.take(got, order, axis=0)


def scatter_sum(whole, axis):
    count = lax.axis_size(axis)
    me = lax.axis_index(axis)
    size = whole.shape[1] // count
    pieces = [
        lax.dynamic_slice_in_dim(whole, ((me + s) % count) * size, size, axis=1)
        for s in range(count)
    ]
    got = exchange(pieces, axis)
    out = got[0]
    for part in got[1:]:
        out = out + part
    return out


def local(inputs, grads, step_size, decay_rate, skip_gain, b_rows, c_rows, doc_lengths):
    length = inputs.shape[0]
    heads = step_size.shape[0]
    width = inputs.shape[1] // heads
    rows = gather_rows(jnp.stack([b_rows, c_rows]), "tensor")
    b_bf = rows[:, 0].reshape(length, -1)
    c_bf = rows[:, 1].reshape(length, -1)
    bmat = b_bf.astype(jnp.float32)
    cmat = c_bf.astype(jnp.float32)
    xs = inputs.astype(jnp.float32).reshape(length, heads, width).transpose(1, 0, 2)
    dys = grads.astype(jnp.float32).reshape(length, heads, width).transpose(1, 0, 2)
    offset = lax.axis_index("context") * length
    ends = jnp.cumsum(doc_lengths)
    starts = ends - doc_lengths
    position = offset + jnp.arange(length, dtype=jnp.int32)
    seg = jnp.sum(
        ((starts[None, :] >= offset) & (starts[None, :] <= position[:, None])).astype(jnp.int32),
        axis=1,
    )
    rate = decay_rate[:, None]
    logc = jnp.cumsum(-step_size * rate, axis=1)
    enter = jnp.exp(logc) * (seg == 0).astype(jnp.float32)[None, :]
    leave = jnp.exp(logc[:, -1:] - logc) * (seg == seg[-1]).astype(jnp.float32)[None, :]
    total = enter[:, -1][:, None, None]
    moved = step_size[:, :, None] * xs
    left_u = leave[:, :, None] * moved
    enter_dy = enter[:, :, None] * dys
    local_state = jnp.einsum("hlp,ln->hpn", left_u, bmat, precision=HIGH)
    local_adj = jnp.einsum("hlp,ln->hpn", enter_dy, cmat, precision=HIGH)

    reach = 3 * lax.axis_size("context") // 16
    low = reach & -reach
    high = reach - low
    assert high > 0 and high & (high - 1) == 0 and low < high
    fwd = (local_state, total)
    bwd = (local_adj, total)
    span = 1
    kept = {}
    while span < high:
        kept[span] = (fwd, bwd)
        got_f, got_b = shift_pair(fwd, bwd, span)
        fwd = (fwd[0] + fwd[1] * got_f[0], fwd[1] * got_f[1])
        bwd = (bwd[0] + bwd[1] * got_b[0], bwd[1] * got_b[1])
        span *= 2
    near_f, near_b = kept[low]
    got = lax.optimization_barrier(
        (
            from_behind(near_f, "context", 1),
            from_behind(fwd[0], "context", low + 1),
            from_behind(near_b, "context", -1),
            from_behind(bwd[0], "context", -low - 1),
        )
    )
    s_in = got[0][0] + got[0][1] * got[1]
    g_in = got[2][0] + got[2][1] * got[3]

    index = jnp.arange(length)
    keep = (index[:, None] >= index[None, :]) & (seg[:, None] == seg[None, :])
    weights = jnp.exp(jnp.where(keep[None], logc[:, :, None] - logc[:, None, :], -1e30))
    scores = jnp.dot(c_bf, b_bf.T, preferred_element_type=jnp.float32)
    mixed = weights * scores[None]
    core_loc = jnp.einsum("hij,hip->hjp", mixed, dys, precision=HIGH)
    pairs = jnp.einsum("hip,hjp->hij", dys, moved, precision=HIGH)
    paired = mixed * pairs
    col_total = jnp.sum(paired, axis=1)
    row_total = jnp.sum(paired, axis=2)
    inner = jnp.cumsum(col_total, axis=1) - (jnp.cumsum(row_total, axis=1) - row_total)
    weighted = jnp.sum(weights * pairs, axis=0)
    gb_loc = jnp.dot(weighted.T, cmat, precision=HIGH)
    gc_loc = jnp.dot(weighted, bmat, precision=HIGH)

    b_adj = jnp.einsum("ln,hpn->hlp", bmat, g_in, precision=HIGH)
    c_state = jnp.einsum("ln,hpn->hlp", cmat, s_in, precision=HIGH)
    core = core_loc + leave[:, :, None] * b_adj
    gx = step_size[:, :, None] * core + skip_gain[:, None, None] * dys
    along = jnp.sum(xs * core, axis=2)
    from_state = enter * jnp.einsum(
        "hij,hi->hj", weights, jnp.sum(dys * c_state, axis=2), precision=HIGH
    )
    from_adj = leave * jnp.einsum(
        "hij,hj->hi", weights, jnp.sum(moved * b_adj, axis=2), precision=HIGH
    )
    both = leave * enter * jnp.sum(g_in * s_in, axis=(1, 2))[:, None]
    grad_step = along * (1.0 + rate * step_size) - rate * (inner + from_state + from_adj + both)
    gb = gb_loc + jnp.einsum("hlp,hpn->ln", left_u, g_in, precision=HIGH)
    gc = gc_loc + jnp.einsum("hlp,hpn->ln", enter_dy, s_in, precision=HIGH)

    grad_x = gx.transpose(1, 0, 2).reshape(length, heads * width)
    grad_bc = scatter_sum(jnp.stack([gb, gc]), "tensor")
    return (grad_x, grad_step, grad_bc[0], grad_bc[1])


def solution(mesh):
    in_specs = (
        P("context", "tensor"),
        P("context", "tensor"),
        P("tensor", "context"),
        P("tensor"),
        P("tensor"),
        P(("context", "tensor"), None),
        P(("context", "tensor"), None),
        P(),
    )
    out_specs = (
        P("context", "tensor"),
        P("tensor", "context"),
        P(("context", "tensor"), None),
        P(("context", "tensor"), None),
    )
    return jax.shard_map(local, mesh=mesh, in_specs=in_specs, out_specs=out_specs, check_vma=False)
```

```python
import jax
import jax.numpy as jnp
from jax import lax
from jax.sharding import PartitionSpec as P

HIGH = lax.Precision.HIGHEST


def from_behind(x, axis, by):
    peers = lax.axis_size(axis)
    pairs = [(i, i + by) for i in range(peers) if 0 <= i + by < peers]
    return lax.ppermute(x, axis, pairs)


def pack(value):
    top = jnp.max(jnp.abs(value), axis=-1, keepdims=True)
    unit = jnp.where(top > 0, top, 1.0) / 32767.0
    return jnp.round(value / unit).astype(jnp.int16), unit


def unpack(packed):
    code, unit = packed
    return code.astype(jnp.float32) * unit


def shift_pair(fwd, bwd, by):
    fwd, bwd = lax.optimization_barrier(((pack(fwd[0]), fwd[1]), (pack(bwd[0]), bwd[1])))
    got_f, got_b = lax.optimization_barrier(
        (from_behind(fwd, "context", by), from_behind(bwd, "context", -by))
    )
    return (unpack(got_f[0]), got_f[1]), (unpack(got_b[0]), got_b[1])


def exchange(pieces, axis):
    count = lax.axis_size(axis)
    pieces = lax.optimization_barrier(pieces)
    got = [
        lax.ppermute(pieces[s], axis, [(i, (i + s) % count) for i in range(count)])
        for s in range(1, count)
    ]
    return [pieces[0]] + list(lax.optimization_barrier(got))


def scatter_sum(whole, axis):
    count = lax.axis_size(axis)
    me = lax.axis_index(axis)
    size = whole.shape[1] // count
    pieces = [
        lax.dynamic_slice_in_dim(whole, ((me + s) % count) * size, size, axis=1)
        for s in range(count)
    ]
    got = exchange(pieces, axis)
    out = got[0]
    for part in got[1:]:
        out = out + part
    return out


def local(inputs, grads, step_size, decay_rate, skip_gain, b_rows, c_rows, doc_lengths):
    length = inputs.shape[0]
    heads = step_size.shape[0]
    width = inputs.shape[1] // heads
    rows = lax.all_gather(jnp.stack([b_rows, c_rows]), "tensor", axis=1, tiled=True)
    b_bf, c_bf = rows[0], rows[1]
    bmat = b_bf.astype(jnp.float32)
    cmat = c_bf.astype(jnp.float32)
    xs = inputs.astype(jnp.float32).reshape(length, heads, width).transpose(1, 0, 2)
    dys = grads.astype(jnp.float32).reshape(length, heads, width).transpose(1, 0, 2)
    offset = lax.axis_index("context") * length
    ends = jnp.cumsum(doc_lengths)
    starts = ends - doc_lengths
    position = offset + jnp.arange(length, dtype=jnp.int32)
    seg = jnp.sum(
        ((starts[None, :] >= offset) & (starts[None, :] <= position[:, None])).astype(jnp.int32),
        axis=1,
    )
    rate = decay_rate[:, None]
    logc = jnp.cumsum(-step_size * rate, axis=1)
    enter = jnp.exp(logc) * (seg == 0).astype(jnp.float32)[None, :]
    leave = jnp.exp(logc[:, -1:] - logc) * (seg == seg[-1]).astype(jnp.float32)[None, :]
    total = enter[:, -1][:, None, None]
    moved = step_size[:, :, None] * xs
    left_u = leave[:, :, None] * moved
    enter_dy = enter[:, :, None] * dys
    local_state = jnp.einsum("hlp,ln->hpn", left_u, bmat, precision=HIGH)
    local_adj = jnp.einsum("hlp,ln->hpn", enter_dy, cmat, precision=HIGH)

    reach = 3 * lax.axis_size("context") // 16
    low = reach & -reach
    high = reach - low
    assert high > 0 and high & (high - 1) == 0 and low < high
    fwd = (local_state, total)
    bwd = (local_adj, total)
    span = 1
    kept = {}
    while span < high:
        kept[span] = (fwd, bwd)
        got_f, got_b = shift_pair(fwd, bwd, span)
        fwd = (fwd[0] + fwd[1] * got_f[0], fwd[1] * got_f[1])
        bwd = (bwd[0] + bwd[1] * got_b[0], bwd[1] * got_b[1])
        span *= 2
    near_f, near_b = kept[low]
    sends = lax.optimization_barrier(
        ((pack(near_f[0]), near_f[1]), pack(fwd[0]), (pack(near_b[0]), near_b[1]), pack(bwd[0]))
    )
    got = lax.optimization_barrier(
        (
            from_behind(sends[0], "context", 1),
            from_behind(sends[1], "context", low + 1),
            from_behind(sends[2], "context", -1),
            from_behind(sends[3], "context", -low - 1),
        )
    )
    s_in = unpack(got[0][0]) + got[0][1] * unpack(got[1])
    g_in = unpack(got[2][0]) + got[2][1] * unpack(got[3])

    index = jnp.arange(length)
    keep = (index[:, None] >= index[None, :]) & (seg[:, None] == seg[None, :])
    weights = jnp.exp(jnp.where(keep[None], logc[:, :, None] - logc[:, None, :], -1e30))
    scores = jnp.dot(c_bf, b_bf.T, preferred_element_type=jnp.float32)
    mixed = weights * scores[None]
    core_loc = jnp.einsum("hij,hip->hjp", mixed, dys, precision=HIGH)
    pairs = jnp.einsum("hip,hjp->hij", dys, moved, precision=HIGH)
    paired = mixed * pairs
    col_total = jnp.sum(paired, axis=1)
    row_total = jnp.sum(paired, axis=2)
    inner = jnp.cumsum(col_total, axis=1) - (jnp.cumsum(row_total, axis=1) - row_total)
    weighted = jnp.sum(weights * pairs, axis=0)
    gb_loc = jnp.dot(weighted.T, cmat, precision=HIGH)
    gc_loc = jnp.dot(weighted, bmat, precision=HIGH)

    b_adj = jnp.einsum("ln,hpn->hlp", bmat, g_in, precision=HIGH)
    c_state = jnp.einsum("ln,hpn->hlp", cmat, s_in, precision=HIGH)
    core = core_loc + leave[:, :, None] * b_adj
    gx = step_size[:, :, None] * core + skip_gain[:, None, None] * dys
    along = jnp.sum(xs * core, axis=2)
    from_state = enter * jnp.einsum(
        "hij,hi->hj", weights, jnp.sum(dys * c_state, axis=2), precision=HIGH
    )
    from_adj = leave * jnp.einsum(
        "hij,hj->hi", weights, jnp.sum(moved * b_adj, axis=2), precision=HIGH
    )
    both = leave * enter * jnp.sum(g_in * s_in, axis=(1, 2))[:, None]
    grad_step = along * (1.0 + rate * step_size) - rate * (inner + from_state + from_adj + both)
    gb = gb_loc + jnp.einsum("hlp,hpn->ln", left_u, g_in, precision=HIGH)
    gc = gc_loc + jnp.einsum("hlp,hpn->ln", enter_dy, s_in, precision=HIGH)

    grad_x = gx.transpose(1, 0, 2).reshape(length, heads * width)
    grad_bc = scatter_sum(jnp.stack([gb, gc]), "tensor")
    return (grad_x, grad_step, grad_bc[0], grad_bc[1])


def solution(mesh):
    in_specs = (
        P("context", "tensor"),
        P("context", "tensor"),
        P("tensor", "context"),
        P("tensor"),
        P("tensor"),
        P(("context", "tensor"), None),
        P(("context", "tensor"), None),
        P(),
    )
    out_specs = (
        P("context", "tensor"),
        P("tensor", "context"),
        P(("context", "tensor"), None),
        P(("context", "tensor"), None),
    )
    return jax.shard_map(local, mesh=mesh, in_specs=in_specs, out_specs=out_specs, check_vma=False)
```

```python
import jax
import jax.numpy as jnp
from jax import lax
from jax.sharding import PartitionSpec as P

HIGH = lax.Precision.HIGHEST


def from_behind(x, axis, by):
    peers = lax.axis_size(axis)
    pairs = [(i, i + by) for i in range(peers) if 0 <= i + by < peers]
    return lax.ppermute(x, axis, pairs)


FLOOR = -150.0


def pack(value, decay):
    top = jnp.max(jnp.abs(value), axis=-1, keepdims=True)
    expo = jnp.maximum(jnp.ceil(jnp.log2(jnp.where(top > 0, top, 1.0))), -100.0)
    code = jnp.clip(jnp.round(value / jnp.exp2(expo - 15.0)), -32767.0, 32767.0).astype(jnp.int16)
    scaled = decay * 64.0
    high = jnp.floor(scaled)
    low = jnp.round((scaled - high) * 16384.0)
    tail = jnp.zeros((1, 128), jnp.float32).at[0, : decay.shape[0]].set(high)
    tail = tail.at[0, decay.shape[0] : 2 * decay.shape[0]].set(low)
    lanes = value.shape[-1]
    return jnp.concatenate(
        [code.reshape(-1, lanes), expo.reshape(-1, lanes).astype(jnp.int16), tail.astype(jnp.int16)]
    )


def unpack(packed, shape):
    body = shape[0] * shape[1]
    code = packed[:body].astype(jnp.float32).reshape(shape)
    expo = packed[body : body + body // shape[2]].astype(jnp.float32).reshape(shape[:2] + (1,))
    tail = packed[-1].astype(jnp.float32)
    decay = (tail[: shape[0]] + tail[shape[0] : 2 * shape[0]] / 16384.0) / 64.0
    return code * jnp.exp2(expo - 15.0), decay


def combine(own, got):
    value = own[0] + jnp.exp(own[1])[:, None, None] * got[0]
    return value, jnp.maximum(own[1] + got[1], FLOOR)


def shift_pair(fwd, bwd, by):
    shape = fwd[0].shape
    fwd, bwd = lax.optimization_barrier((pack(*fwd), pack(*bwd)))
    got_f, got_b = lax.optimization_barrier(
        (from_behind(fwd, "context", by), from_behind(bwd, "context", -by))
    )
    return unpack(got_f, shape), unpack(got_b, shape)


def exchange(pieces, axis):
    count = lax.axis_size(axis)
    pieces = lax.optimization_barrier(pieces)
    got = [
        lax.ppermute(pieces[s], axis, [(i, (i + s) % count) for i in range(count)])
        for s in range(1, count)
    ]
    return [pieces[0]] + list(lax.optimization_barrier(got))


def scatter_sum(whole, axis):
    count = lax.axis_size(axis)
    me = lax.axis_index(axis)
    size = whole.shape[1] // count
    pieces = [
        lax.dynamic_slice_in_dim(whole, ((me + s) % count) * size, size, axis=1)
        for s in range(count)
    ]
    got = exchange(pieces, axis)
    out = got[0]
    for part in got[1:]:
        out = out + part
    return out


def local(inputs, grads, step_size, decay_rate, skip_gain, b_rows, c_rows, doc_lengths):
    length = inputs.shape[0]
    heads = step_size.shape[0]
    width = inputs.shape[1] // heads
    rows = lax.all_gather(jnp.stack([b_rows, c_rows]), "tensor", axis=1, tiled=True)
    b_bf, c_bf = rows[0], rows[1]
    bmat = b_bf.astype(jnp.float32)
    cmat = c_bf.astype(jnp.float32)
    xs = inputs.astype(jnp.float32).reshape(length, heads, width).transpose(1, 0, 2)
    dys = grads.astype(jnp.float32).reshape(length, heads, width).transpose(1, 0, 2)
    offset = lax.axis_index("context") * length
    ends = jnp.cumsum(doc_lengths)
    starts = ends - doc_lengths
    position = offset + jnp.arange(length, dtype=jnp.int32)
    seg = jnp.sum(
        ((starts[None, :] >= offset) & (starts[None, :] <= position[:, None])).astype(jnp.int32),
        axis=1,
    )
    rate = decay_rate[:, None]
    logc = jnp.cumsum(-step_size * rate, axis=1)
    enter = jnp.exp(logc) * (seg == 0).astype(jnp.float32)[None, :]
    leave = jnp.exp(logc[:, -1:] - logc) * (seg == seg[-1]).astype(jnp.float32)[None, :]
    moved = step_size[:, :, None] * xs
    left_u = leave[:, :, None] * moved
    enter_dy = enter[:, :, None] * dys
    local_state = jnp.einsum("hlp,ln->hpn", left_u, bmat, precision=HIGH)
    local_adj = jnp.einsum("hlp,ln->hpn", enter_dy, cmat, precision=HIGH)

    reach = 3 * lax.axis_size("context") // 16
    low = reach & -reach
    high = reach - low
    assert high > 0 and high & (high - 1) == 0 and low < high
    shape = local_state.shape
    decay = jnp.where(seg[-1] == 0, jnp.maximum(logc[:, -1], FLOOR), FLOOR)
    fwd = (local_state, decay)
    bwd = (local_adj, decay)
    span = 1
    kept = {}
    while span < high:
        kept[span] = (fwd, bwd)
        got_f, got_b = shift_pair(fwd, bwd, span)
        fwd = combine(fwd, got_f)
        bwd = combine(bwd, got_b)
        span *= 2
    near_f, near_b = kept[low]
    sends = lax.optimization_barrier((pack(*near_f), pack(*fwd), pack(*near_b), pack(*bwd)))
    got = lax.optimization_barrier(
        (
            from_behind(sends[0], "context", 1),
            from_behind(sends[1], "context", low + 1),
            from_behind(sends[2], "context", -1),
            from_behind(sends[3], "context", -low - 1),
        )
    )
    got = [unpack(g, shape) for g in got]
    s_in = combine(got[0], got[1])[0]
    g_in = combine(got[2], got[3])[0]

    index = jnp.arange(length)
    keep = (index[:, None] >= index[None, :]) & (seg[:, None] == seg[None, :])
    weights = jnp.exp(jnp.where(keep[None], logc[:, :, None] - logc[:, None, :], -1e30))
    scores = jnp.dot(c_bf, b_bf.T, preferred_element_type=jnp.float32)
    mixed = weights * scores[None]
    core_loc = jnp.einsum("hij,hip->hjp", mixed, dys, precision=HIGH)
    pairs = jnp.einsum("hip,hjp->hij", dys, moved, precision=HIGH)
    paired = mixed * pairs
    col_total = jnp.sum(paired, axis=1)
    row_total = jnp.sum(paired, axis=2)
    inner = jnp.cumsum(col_total, axis=1) - (jnp.cumsum(row_total, axis=1) - row_total)
    weighted = jnp.sum(weights * pairs, axis=0)
    gb_loc = jnp.dot(weighted.T, cmat, precision=HIGH)
    gc_loc = jnp.dot(weighted, bmat, precision=HIGH)

    b_adj = jnp.einsum("ln,hpn->hlp", bmat, g_in, precision=HIGH)
    c_state = jnp.einsum("ln,hpn->hlp", cmat, s_in, precision=HIGH)
    core = core_loc + leave[:, :, None] * b_adj
    gx = step_size[:, :, None] * core + skip_gain[:, None, None] * dys
    along = jnp.sum(xs * core, axis=2)
    from_state = enter * jnp.einsum(
        "hij,hi->hj", weights, jnp.sum(dys * c_state, axis=2), precision=HIGH
    )
    from_adj = leave * jnp.einsum(
        "hij,hj->hi", weights, jnp.sum(moved * b_adj, axis=2), precision=HIGH
    )
    both = leave * enter * jnp.sum(g_in * s_in, axis=(1, 2))[:, None]
    grad_step = along * (1.0 + rate * step_size) - rate * (inner + from_state + from_adj + both)
    gb = gb_loc + jnp.einsum("hlp,hpn->ln", left_u, g_in, precision=HIGH)
    gc = gc_loc + jnp.einsum("hlp,hpn->ln", enter_dy, s_in, precision=HIGH)

    grad_x = gx.transpose(1, 0, 2).reshape(length, heads * width)
    grad_bc = scatter_sum(jnp.stack([gb, gc]), "tensor")
    return (grad_x, grad_step, grad_bc[0], grad_bc[1])


def solution(mesh):
    in_specs = (
        P("context", "tensor"),
        P("context", "tensor"),
        P("tensor", "context"),
        P("tensor"),
        P("tensor"),
        P(("context", "tensor"), None),
        P(("context", "tensor"), None),
        P(),
    )
    out_specs = (
        P("context", "tensor"),
        P("tensor", "context"),
        P(("context", "tensor"), None),
        P(("context", "tensor"), None),
    )
    return jax.shard_map(local, mesh=mesh, in_specs=in_specs, out_specs=out_specs, check_vma=False)
```

```python
import jax
import jax.numpy as jnp
from jax import lax
from jax.sharding import PartitionSpec as P

HIGH = lax.Precision.HIGHEST


def from_behind(x, axis, by):
    peers = lax.axis_size(axis)
    pairs = [(i, i + by) for i in range(peers) if 0 <= i + by < peers]
    return lax.ppermute(x, axis, pairs)


FLOOR = -150.0


def pack(value, decay):
    top = jnp.max(jnp.abs(value), axis=-1, keepdims=True)
    expo = jnp.maximum(jnp.ceil(jnp.log2(jnp.where(top > 0, top, 1.0))), -100.0)
    code = jnp.clip(jnp.round(value / jnp.exp2(expo - 15.0)), -32767.0, 32767.0).astype(jnp.int16)
    scaled = decay * 64.0
    high = jnp.floor(scaled)
    low = jnp.round((scaled - high) * 16384.0)
    lanes = value.shape[-1]
    tail = jnp.concatenate([high, low, jnp.zeros((lanes - 2 * decay.shape[0],), jnp.float32)])[None]
    return jnp.concatenate(
        [code.reshape(-1, lanes), expo.reshape(-1, lanes).astype(jnp.int16), tail.astype(jnp.int16)]
    )


def unpack(packed, shape):
    body = shape[0] * shape[1]
    code = packed[:body].astype(jnp.float32).reshape(shape)
    expo = packed[body : body + body // shape[2]].astype(jnp.float32).reshape(shape[:2] + (1,))
    tail = packed[-1].astype(jnp.float32)
    decay = (tail[: shape[0]] + tail[shape[0] : 2 * shape[0]] / 16384.0) / 64.0
    return code * jnp.exp2(expo - 15.0), decay


def combine(own, got):
    value = own[0] + jnp.exp(own[1])[:, None, None] * got[0]
    return value, jnp.maximum(own[1] + got[1], FLOOR)


def shift_pair(fwd, bwd, by):
    shape = fwd[0].shape
    fwd, bwd = lax.optimization_barrier((pack(*fwd), pack(*bwd)))
    got_f, got_b = lax.optimization_barrier(
        (from_behind(fwd, "context", by), from_behind(bwd, "context", -by))
    )
    return unpack(got_f, shape), unpack(got_b, shape)


def exchange(pieces, axis):
    count = lax.axis_size(axis)
    pieces = lax.optimization_barrier(pieces)
    got = [
        lax.ppermute(pieces[s], axis, [(i, (i + s) % count) for i in range(count)])
        for s in range(1, count)
    ]
    return [pieces[0]] + list(lax.optimization_barrier(got))


def scatter_sum(whole, axis):
    count = lax.axis_size(axis)
    size = whole.shape[1] // count
    parts = whole.reshape(whole.shape[0], count, size, whole.shape[2]).transpose(1, 0, 2, 3)
    got = lax.all_to_all(parts, axis, 0, 0, tiled=True)
    return jnp.sum(got, axis=0)


def scatter_sum_by_permutes(whole, axis):
    count = lax.axis_size(axis)
    me = lax.axis_index(axis)
    size = whole.shape[1] // count
    pieces = [
        lax.dynamic_slice_in_dim(whole, ((me + s) % count) * size, size, axis=1)
        for s in range(count)
    ]
    got = exchange(pieces, axis)
    out = got[0]
    for part in got[1:]:
        out = out + part
    return out


def local(inputs, grads, step_size, decay_rate, skip_gain, b_rows, c_rows, doc_lengths):
    length = inputs.shape[0]
    heads = step_size.shape[0]
    width = inputs.shape[1] // heads
    count = lax.axis_size("tensor")
    piece = jnp.stack([b_rows, c_rows])
    rows = lax.all_to_all(jnp.broadcast_to(piece, (count,) + piece.shape), "tensor", 0, 0, tiled=True)
    b_bf = rows[:, 0].reshape(length, -1)
    c_bf = rows[:, 1].reshape(length, -1)
    bmat = b_bf.astype(jnp.float32)
    cmat = c_bf.astype(jnp.float32)
    xs = inputs.astype(jnp.float32).reshape(length, heads, width).transpose(1, 0, 2)
    dys = grads.astype(jnp.float32).reshape(length, heads, width).transpose(1, 0, 2)
    offset = lax.axis_index("context") * length
    ends = jnp.cumsum(doc_lengths)
    starts = ends - doc_lengths
    position = offset + jnp.arange(length, dtype=jnp.int32)
    seg = jnp.sum(
        ((starts[None, :] >= offset) & (starts[None, :] <= position[:, None])).astype(jnp.int32),
        axis=1,
    )
    rate = decay_rate[:, None]
    logc = jnp.cumsum(-step_size * rate, axis=1)
    enter = jnp.exp(logc) * (seg == 0).astype(jnp.float32)[None, :]
    leave = jnp.exp(logc[:, -1:] - logc) * (seg == seg[-1]).astype(jnp.float32)[None, :]
    moved = step_size[:, :, None] * xs
    left_u = leave[:, :, None] * moved
    enter_dy = enter[:, :, None] * dys
    local_state = jnp.einsum("hlp,ln->hpn", left_u, bmat, precision=HIGH)
    local_adj = jnp.einsum("hlp,ln->hpn", enter_dy, cmat, precision=HIGH)

    reach = 3 * lax.axis_size("context") // 16
    low = reach & -reach
    high = reach - low
    assert high > 0 and high & (high - 1) == 0 and low < high
    shape = local_state.shape
    decay = jnp.where(seg[-1] == 0, jnp.maximum(logc[:, -1], FLOOR), FLOOR)
    fwd = (local_state, decay)
    bwd = (local_adj, decay)
    span = 1
    kept = {}
    while span < high:
        kept[span] = (fwd, bwd)
        got_f, got_b = shift_pair(fwd, bwd, span)
        fwd = combine(fwd, got_f)
        bwd = combine(bwd, got_b)
        span *= 2
    near_f, near_b = kept[low]
    sends = lax.optimization_barrier((pack(*near_f), pack(*fwd), pack(*near_b), pack(*bwd)))
    got = lax.optimization_barrier(
        (
            from_behind(sends[0], "context", 1),
            from_behind(sends[1], "context", low + 1),
            from_behind(sends[2], "context", -1),
            from_behind(sends[3], "context", -low - 1),
        )
    )
    got = [unpack(g, shape) for g in got]
    s_in = combine(got[0], got[1])[0]
    g_in = combine(got[2], got[3])[0]

    index = jnp.arange(length)
    keep = (index[:, None] >= index[None, :]) & (seg[:, None] == seg[None, :])
    weights = jnp.exp(jnp.where(keep[None], logc[:, :, None] - logc[:, None, :], -1e30))
    scores = jnp.dot(c_bf, b_bf.T, preferred_element_type=jnp.float32)
    mixed = weights * scores[None]
    core_loc = jnp.einsum("hij,hip->hjp", mixed, dys, precision=HIGH)
    pairs = jnp.einsum("hip,hjp->hij", dys, moved, precision=HIGH)
    paired = mixed * pairs
    col_total = jnp.sum(paired, axis=1)
    row_total = jnp.sum(paired, axis=2)
    inner = jnp.cumsum(col_total, axis=1) - (jnp.cumsum(row_total, axis=1) - row_total)
    weighted = jnp.sum(weights * pairs, axis=0)
    gb_loc = jnp.dot(weighted.T, cmat, precision=HIGH)
    gc_loc = jnp.dot(weighted, bmat, precision=HIGH)

    b_adj = jnp.einsum("ln,hpn->hlp", bmat, g_in, precision=HIGH)
    c_state = jnp.einsum("ln,hpn->hlp", cmat, s_in, precision=HIGH)
    core = core_loc + leave[:, :, None] * b_adj
    gx = step_size[:, :, None] * core + skip_gain[:, None, None] * dys
    along = jnp.sum(xs * core, axis=2)
    from_state = enter * jnp.einsum(
        "hij,hi->hj", weights, jnp.sum(dys * c_state, axis=2), precision=HIGH
    )
    from_adj = leave * jnp.einsum(
        "hij,hj->hi", weights, jnp.sum(moved * b_adj, axis=2), precision=HIGH
    )
    both = leave * enter * jnp.sum(g_in * s_in, axis=(1, 2))[:, None]
    grad_step = along * (1.0 + rate * step_size) - rate * (inner + from_state + from_adj + both)
    gb = gb_loc + jnp.einsum("hlp,hpn->ln", left_u, g_in, precision=HIGH)
    gc = gc_loc + jnp.einsum("hlp,hpn->ln", enter_dy, s_in, precision=HIGH)

    grad_x = gx.transpose(1, 0, 2).reshape(length, heads * width)
    grad_bc = scatter_sum(jnp.stack([gb, gc]), "tensor")
    return (grad_x, grad_step, grad_bc[0], grad_bc[1])


def solution(mesh):
    in_specs = (
        P("context", "tensor"),
        P("context", "tensor"),
        P("tensor", "context"),
        P("tensor"),
        P("tensor"),
        P(("context", "tensor"), None),
        P(("context", "tensor"), None),
        P(),
    )
    out_specs = (
        P("context", "tensor"),
        P("tensor", "context"),
        P(("context", "tensor"), None),
        P(("context", "tensor"), None),
    )
    return jax.shard_map(local, mesh=mesh, in_specs=in_specs, out_specs=out_specs, check_vma=False)
```

```python
import jax
import jax.numpy as jnp
from jax import lax
from jax.sharding import PartitionSpec as P

HIGH = lax.Precision.HIGHEST


def from_behind(x, axis, by):
    peers = lax.axis_size(axis)
    pairs = [(i, i + by) for i in range(peers) if 0 <= i + by < peers]
    return lax.ppermute(x, axis, pairs)


FLOOR = -150.0


def pack(value, decay):
    top = jnp.max(jnp.abs(value), axis=-1, keepdims=True)
    expo = jnp.maximum(jnp.ceil(jnp.log2(jnp.where(top > 0, top, 1.0))), -100.0)
    code = jnp.clip(jnp.round(value / jnp.exp2(expo - 15.0)), -32767.0, 32767.0).astype(jnp.int16)
    scaled = decay * 64.0
    high = jnp.floor(scaled)
    low = jnp.round((scaled - high) * 16384.0)
    lanes = value.shape[-1]
    tail = jnp.concatenate([high, low, jnp.zeros((lanes - 2 * decay.shape[0],), jnp.float32)])[None]
    return jnp.concatenate(
        [code.reshape(-1, lanes), expo.reshape(-1, lanes).astype(jnp.int16), tail.astype(jnp.int16)]
    )


def unpack(packed, shape):
    body = shape[0] * shape[1]
    code = packed[:body].astype(jnp.float32).reshape(shape)
    expo = packed[body : body + body // shape[2]].astype(jnp.float32).reshape(shape[:2] + (1,))
    tail = packed[-1].astype(jnp.float32)
    decay = (tail[: shape[0]] + tail[shape[0] : 2 * shape[0]] / 16384.0) / 64.0
    return code * jnp.exp2(expo - 15.0), decay


def combine(own, got):
    value = own[0] + jnp.exp(own[1])[:, None, None] * got[0]
    return value, jnp.maximum(own[1] + got[1], FLOOR)


def shift_pair(fwd, bwd, by):
    shape = fwd[0].shape
    fwd, bwd = lax.optimization_barrier((pack(*fwd), pack(*bwd)))
    got_f, got_b = lax.optimization_barrier(
        (from_behind(fwd, "context", by), from_behind(bwd, "context", -by))
    )
    return unpack(got_f, shape), unpack(got_b, shape)


def exchange(pieces, axis):
    count = lax.axis_size(axis)
    pieces = lax.optimization_barrier(pieces)
    got = [
        lax.ppermute(pieces[s], axis, [(i, (i + s) % count) for i in range(count)])
        for s in range(1, count)
    ]
    return [pieces[0]] + list(lax.optimization_barrier(got))


def scatter_sum(whole, axis):
    count = lax.axis_size(axis)
    size = whole.shape[1] // count
    parts = whole.reshape(whole.shape[0], count, size, whole.shape[2]).transpose(1, 0, 2, 3)
    got = lax.all_to_all(parts, axis, 0, 0, tiled=True)
    return jnp.sum(got, axis=0)


def scatter_sum_by_permutes(whole, axis):
    count = lax.axis_size(axis)
    me = lax.axis_index(axis)
    size = whole.shape[1] // count
    pieces = [
        lax.dynamic_slice_in_dim(whole, ((me + s) % count) * size, size, axis=1)
        for s in range(count)
    ]
    got = exchange(pieces, axis)
    out = got[0]
    for part in got[1:]:
        out = out + part
    return out


def local(inputs, grads, step_size, decay_rate, skip_gain, b_rows, c_rows, doc_lengths):
    length = inputs.shape[0]
    heads = step_size.shape[0]
    width = inputs.shape[1] // heads
    count = lax.axis_size("tensor")
    piece = jnp.stack([b_rows, c_rows])
    rows = lax.all_to_all(jnp.broadcast_to(piece, (count,) + piece.shape), "tensor", 0, 0, tiled=True)
    b_bf = rows[:, 0].reshape(length, -1)
    c_bf = rows[:, 1].reshape(length, -1)
    bmat = b_bf.astype(jnp.float32)
    cmat = c_bf.astype(jnp.float32)
    xs = inputs.astype(jnp.float32).reshape(length, heads, width).transpose(1, 0, 2)
    dys = grads.astype(jnp.float32).reshape(length, heads, width).transpose(1, 0, 2)
    offset = lax.axis_index("context") * length
    ends = jnp.cumsum(doc_lengths)
    starts = ends - doc_lengths
    position = offset + jnp.arange(length, dtype=jnp.int32)
    seg = jnp.sum(
        ((starts[None, :] >= offset) & (starts[None, :] <= position[:, None])).astype(jnp.int32),
        axis=1,
    )
    rate = decay_rate[:, None]
    logc = jnp.cumsum(-step_size * rate, axis=1)
    enter = jnp.exp(logc) * (seg == 0).astype(jnp.float32)[None, :]
    leave = jnp.exp(logc[:, -1:] - logc) * (seg == seg[-1]).astype(jnp.float32)[None, :]
    moved = step_size[:, :, None] * xs
    left_u = leave[:, :, None] * moved
    enter_dy = enter[:, :, None] * dys
    local_state = jnp.einsum("hlp,ln->hpn", left_u, bmat, precision=HIGH)
    local_adj = jnp.einsum("hlp,ln->hpn", enter_dy, cmat, precision=HIGH)

    reach = 3 * lax.axis_size("context") // 16
    low = reach & -reach
    high = reach - low
    assert high > 0 and high & (high - 1) == 0 and low < high
    spans = []
    while 2 ** len(spans) < high:
        spans.append(2 ** len(spans))
    decay = jnp.where(seg[-1] == 0, jnp.maximum(logc[:, -1], FLOOR), FLOOR)
    groups = 2
    size = heads // groups
    live = []
    for g in range(groups):
        part = slice(g * size, (g + 1) * size)
        live.append({"fwd": (local_state[part], decay[part]), "bwd": (local_adj[part], decay[part])})
    shape = live[0]["fwd"][0].shape
    for step in range(len(spans) + groups):
        sends = []
        for g in range(groups):
            r = step - g
            if 0 <= r < len(spans):
                own = live[g]
                own["kept" + str(spans[r])] = (own["fwd"], own["bwd"])
                sends.append((g, r, pack(*own["fwd"]), spans[r]))
                sends.append((g, r, pack(*own["bwd"]), -spans[r]))
            elif r == len(spans):
                own = live[g]
                near_f, near_b = own["kept" + str(low)]
                sends.append((g, r, pack(*near_f), 1))
                sends.append((g, r, pack(*own["fwd"]), low + 1))
                sends.append((g, r, pack(*near_b), -1))
                sends.append((g, r, pack(*own["bwd"]), -low - 1))
        packed = lax.optimization_barrier([item[2] for item in sends])
        got = lax.optimization_barrier(
            [from_behind(p, "context", item[3]) for p, item in zip(packed, sends)]
        )
        got = [unpack(x, shape) for x in got]
        for g in range(groups):
            mine = [x for x, item in zip(got, sends) if item[0] == g]
            r = step - g
            if 0 <= r < len(spans):
                live[g]["fwd"] = combine(live[g]["fwd"], mine[0])
                live[g]["bwd"] = combine(live[g]["bwd"], mine[1])
            elif r == len(spans):
                live[g]["s_in"] = combine(mine[0], mine[1])[0]
                live[g]["g_in"] = combine(mine[2], mine[3])[0]
    s_in = jnp.concatenate([own["s_in"] for own in live])
    g_in = jnp.concatenate([own["g_in"] for own in live])

    index = jnp.arange(length)
    keep = (index[:, None] >= index[None, :]) & (seg[:, None] == seg[None, :])
    weights = jnp.exp(jnp.where(keep[None], logc[:, :, None] - logc[:, None, :], -1e30))
    scores = jnp.dot(c_bf, b_bf.T, preferred_element_type=jnp.float32)
    mixed = weights * scores[None]
    core_loc = jnp.einsum("hij,hip->hjp", mixed, dys, precision=HIGH)
    pairs = jnp.einsum("hip,hjp->hij", dys, moved, precision=HIGH)
    paired = mixed * pairs
    col_total = jnp.sum(paired, axis=1)
    row_total = jnp.sum(paired, axis=2)
    inner = jnp.cumsum(col_total, axis=1) - (jnp.cumsum(row_total, axis=1) - row_total)
    weighted = jnp.sum(weights * pairs, axis=0)
    gb_loc = jnp.dot(weighted.T, cmat, precision=HIGH)
    gc_loc = jnp.dot(weighted, bmat, precision=HIGH)

    b_adj = jnp.einsum("ln,hpn->hlp", bmat, g_in, precision=HIGH)
    c_state = jnp.einsum("ln,hpn->hlp", cmat, s_in, precision=HIGH)
    core = core_loc + leave[:, :, None] * b_adj
    gx = step_size[:, :, None] * core + skip_gain[:, None, None] * dys
    along = jnp.sum(xs * core, axis=2)
    from_state = enter * jnp.einsum(
        "hij,hi->hj", weights, jnp.sum(dys * c_state, axis=2), precision=HIGH
    )
    from_adj = leave * jnp.einsum(
        "hij,hj->hi", weights, jnp.sum(moved * b_adj, axis=2), precision=HIGH
    )
    both = leave * enter * jnp.sum(g_in * s_in, axis=(1, 2))[:, None]
    grad_step = along * (1.0 + rate * step_size) - rate * (inner + from_state + from_adj + both)
    gb = gb_loc + jnp.einsum("hlp,hpn->ln", left_u, g_in, precision=HIGH)
    gc = gc_loc + jnp.einsum("hlp,hpn->ln", enter_dy, s_in, precision=HIGH)

    grad_x = gx.transpose(1, 0, 2).reshape(length, heads * width)
    grad_bc = scatter_sum(jnp.stack([gb, gc]), "tensor")
    return (grad_x, grad_step, grad_bc[0], grad_bc[1])


def solution(mesh):
    in_specs = (
        P("context", "tensor"),
        P("context", "tensor"),
        P("tensor", "context"),
        P("tensor"),
        P("tensor"),
        P(("context", "tensor"), None),
        P(("context", "tensor"), None),
        P(),
    )
    out_specs = (
        P("context", "tensor"),
        P("tensor", "context"),
        P(("context", "tensor"), None),
        P(("context", "tensor"), None),
    )
    return jax.shard_map(local, mesh=mesh, in_specs=in_specs, out_specs=out_specs, check_vma=False)
```

```python
import jax
import jax.numpy as jnp
from jax import lax
from jax.sharding import PartitionSpec as P

HIGH = lax.Precision.HIGHEST


def from_behind(x, axis, by):
    peers = lax.axis_size(axis)
    pairs = [(i, i + by) for i in range(peers) if 0 <= i + by < peers]
    return lax.ppermute(x, axis, pairs)


def around(x, axis, by):
    peers = lax.axis_size(axis)
    return lax.ppermute(x, axis, [(i, (i + by) % peers) for i in range(peers)])


def arrived(got, axis, by):
    peers = lax.axis_size(axis)
    source = lax.axis_index(axis) - by
    real = (source >= 0) & (source < peers)
    return jnp.where(real, got[0], 0.0), jnp.where(real, got[1], 0.0)


FLOOR = -150.0


def pack(value, decay):
    top = jnp.max(jnp.abs(value), axis=-1, keepdims=True)
    expo = jnp.maximum(jnp.ceil(jnp.log2(jnp.where(top > 0, top, 1.0))), -100.0)
    code = jnp.clip(jnp.round(value / jnp.exp2(expo - 15.0)), -32767.0, 32767.0).astype(jnp.int16)
    scaled = decay * 64.0
    high = jnp.floor(scaled)
    low = jnp.round((scaled - high) * 16384.0)
    lanes = value.shape[-1]
    tail = jnp.concatenate([high, low, jnp.zeros((lanes - 2 * decay.shape[0],), jnp.float32)])[None]
    return jnp.concatenate(
        [code.reshape(-1, lanes), expo.reshape(-1, lanes).astype(jnp.int16), tail.astype(jnp.int16)]
    )


def unpack(packed, shape):
    body = shape[0] * shape[1]
    code = packed[:body].astype(jnp.float32).reshape(shape)
    expo = packed[body : body + body // shape[2]].astype(jnp.float32).reshape(shape[:2] + (1,))
    tail = packed[-1].astype(jnp.float32)
    decay = (tail[: shape[0]] + tail[shape[0] : 2 * shape[0]] / 16384.0) / 64.0
    return code * jnp.exp2(expo - 15.0), decay


def combine(own, got):
    value = own[0] + jnp.exp(own[1])[:, None, None] * got[0]
    return value, jnp.maximum(own[1] + got[1], FLOOR)


def shift_pair(fwd, bwd, by):
    shape = fwd[0].shape
    fwd, bwd = lax.optimization_barrier((pack(*fwd), pack(*bwd)))
    got_f, got_b = lax.optimization_barrier(
        (around(fwd, "context", by), around(bwd, "context", -by))
    )
    return (
        arrived(unpack(got_f, shape), "context", by),
        arrived(unpack(got_b, shape), "context", -by),
    )


def exchange(pieces, axis):
    count = lax.axis_size(axis)
    pieces = lax.optimization_barrier(pieces)
    got = [
        lax.ppermute(pieces[s], axis, [(i, (i + s) % count) for i in range(count)])
        for s in range(1, count)
    ]
    return [pieces[0]] + list(lax.optimization_barrier(got))


def scatter_sum(whole, axis):
    count = lax.axis_size(axis)
    size = whole.shape[1] // count
    parts = whole.reshape(whole.shape[0], count, size, whole.shape[2]).transpose(1, 0, 2, 3)
    got = lax.all_to_all(parts, axis, 0, 0, tiled=True)
    return jnp.sum(got, axis=0)


def scatter_sum_by_permutes(whole, axis):
    count = lax.axis_size(axis)
    me = lax.axis_index(axis)
    size = whole.shape[1] // count
    pieces = [
        lax.dynamic_slice_in_dim(whole, ((me + s) % count) * size, size, axis=1)
        for s in range(count)
    ]
    got = exchange(pieces, axis)
    out = got[0]
    for part in got[1:]:
        out = out + part
    return out


def local(inputs, grads, step_size, decay_rate, skip_gain, b_rows, c_rows, doc_lengths):
    length = inputs.shape[0]
    heads = step_size.shape[0]
    width = inputs.shape[1] // heads
    count = lax.axis_size("tensor")
    piece = jnp.stack([b_rows, c_rows])
    rows = lax.all_to_all(jnp.broadcast_to(piece, (count,) + piece.shape), "tensor", 0, 0, tiled=True)
    b_bf = rows[:, 0].reshape(length, -1)
    c_bf = rows[:, 1].reshape(length, -1)
    bmat = b_bf.astype(jnp.float32)
    cmat = c_bf.astype(jnp.float32)
    xs = inputs.astype(jnp.float32).reshape(length, heads, width).transpose(1, 0, 2)
    dys = grads.astype(jnp.float32).reshape(length, heads, width).transpose(1, 0, 2)
    offset = lax.axis_index("context") * length
    ends = jnp.cumsum(doc_lengths)
    starts = ends - doc_lengths
    position = offset + jnp.arange(length, dtype=jnp.int32)
    seg = jnp.sum(
        ((starts[None, :] >= offset) & (starts[None, :] <= position[:, None])).astype(jnp.int32),
        axis=1,
    )
    rate = decay_rate[:, None]
    logc = jnp.cumsum(-step_size * rate, axis=1)
    enter = jnp.exp(logc) * (seg == 0).astype(jnp.float32)[None, :]
    leave = jnp.exp(logc[:, -1:] - logc) * (seg == seg[-1]).astype(jnp.float32)[None, :]
    moved = step_size[:, :, None] * xs
    left_u = leave[:, :, None] * moved
    enter_dy = enter[:, :, None] * dys
    local_state = jnp.einsum("hlp,ln->hpn", left_u, bmat, precision=HIGH)
    local_adj = jnp.einsum("hlp,ln->hpn", enter_dy, cmat, precision=HIGH)

    reach = 3 * lax.axis_size("context") // 16
    low = reach & -reach
    high = reach - low
    assert high > 0 and high & (high - 1) == 0 and low < high
    shape = local_state.shape
    decay = jnp.where(seg[-1] == 0, jnp.maximum(logc[:, -1], FLOOR), FLOOR)
    fwd = (local_state, decay)
    bwd = (local_adj, decay)
    span = 1
    kept = {}
    while span < high:
        kept[span] = (fwd, bwd)
        got_f, got_b = shift_pair(fwd, bwd, span)
        fwd = combine(fwd, got_f)
        bwd = combine(bwd, got_b)
        span *= 2
    near_f, near_b = kept[low]
    sends = lax.optimization_barrier((pack(*near_f), pack(*fwd), pack(*near_b), pack(*bwd)))
    moves = (1, low + 1, -1, -low - 1)
    got = lax.optimization_barrier(
        tuple(around(p, "context", by) for p, by in zip(sends, moves))
    )
    got = [arrived(unpack(g, shape), "context", by) for g, by in zip(got, moves)]
    s_in = combine(got[0], got[1])[0]
    g_in = combine(got[2], got[3])[0]

    index = jnp.arange(length)
    keep = (index[:, None] >= index[None, :]) & (seg[:, None] == seg[None, :])
    weights = jnp.exp(jnp.where(keep[None], logc[:, :, None] - logc[:, None, :], -1e30))
    scores = jnp.dot(c_bf, b_bf.T, preferred_element_type=jnp.float32)
    mixed = weights * scores[None]
    core_loc = jnp.einsum("hij,hip->hjp", mixed, dys, precision=HIGH)
    pairs = jnp.einsum("hip,hjp->hij", dys, moved, precision=HIGH)
    paired = mixed * pairs
    col_total = jnp.sum(paired, axis=1)
    row_total = jnp.sum(paired, axis=2)
    inner = jnp.cumsum(col_total, axis=1) - (jnp.cumsum(row_total, axis=1) - row_total)
    weighted = jnp.sum(weights * pairs, axis=0)
    gb_loc = jnp.dot(weighted.T, cmat, precision=HIGH)
    gc_loc = jnp.dot(weighted, bmat, precision=HIGH)

    b_adj = jnp.einsum("ln,hpn->hlp", bmat, g_in, precision=HIGH)
    c_state = jnp.einsum("ln,hpn->hlp", cmat, s_in, precision=HIGH)
    core = core_loc + leave[:, :, None] * b_adj
    gx = step_size[:, :, None] * core + skip_gain[:, None, None] * dys
    along = jnp.sum(xs * core, axis=2)
    from_state = enter * jnp.einsum(
        "hij,hi->hj", weights, jnp.sum(dys * c_state, axis=2), precision=HIGH
    )
    from_adj = leave * jnp.einsum(
        "hij,hj->hi", weights, jnp.sum(moved * b_adj, axis=2), precision=HIGH
    )
    both = leave * enter * jnp.sum(g_in * s_in, axis=(1, 2))[:, None]
    grad_step = along * (1.0 + rate * step_size) - rate * (inner + from_state + from_adj + both)
    gb = gb_loc + jnp.einsum("hlp,hpn->ln", left_u, g_in, precision=HIGH)
    gc = gc_loc + jnp.einsum("hlp,hpn->ln", enter_dy, s_in, precision=HIGH)

    grad_x = gx.transpose(1, 0, 2).reshape(length, heads * width)
    grad_bc = scatter_sum(jnp.stack([gb, gc]), "tensor")
    return (grad_x, grad_step, grad_bc[0], grad_bc[1])


def solution(mesh):
    in_specs = (
        P("context", "tensor"),
        P("context", "tensor"),
        P("tensor", "context"),
        P("tensor"),
        P("tensor"),
        P(("context", "tensor"), None),
        P(("context", "tensor"), None),
        P(),
    )
    out_specs = (
        P("context", "tensor"),
        P("tensor", "context"),
        P(("context", "tensor"), None),
        P(("context", "tensor"), None),
    )
    return jax.shard_map(local, mesh=mesh, in_specs=in_specs, out_specs=out_specs, check_vma=False)
```

```python
import jax
import jax.numpy as jnp
from jax import lax
from jax.sharding import PartitionSpec as P

HIGH = lax.Precision.HIGHEST


def from_behind(x, axis, by):
    peers = lax.axis_size(axis)
    pairs = [(i, i + by) for i in range(peers) if 0 <= i + by < peers]
    return lax.ppermute(x, axis, pairs)


FLOOR = -150.0


def pack(value, decay):
    top = jnp.max(jnp.abs(value), axis=-1, keepdims=True)
    expo = jnp.maximum(jnp.ceil(jnp.log2(jnp.where(top > 0, top, 1.0))), -100.0)
    code = jnp.clip(jnp.round(value / jnp.exp2(expo - 15.0)), -32767.0, 32767.0).astype(jnp.int16)
    scaled = decay * 64.0
    high = jnp.floor(scaled)
    low = jnp.round((scaled - high) * 16384.0)
    lanes = value.shape[-1]
    tail = jnp.concatenate([high, low, jnp.zeros((lanes - 2 * decay.shape[0],), jnp.float32)])[None]
    return jnp.concatenate(
        [code.reshape(-1, lanes), expo.reshape(-1, lanes).astype(jnp.int16), tail.astype(jnp.int16)]
    )


def unpack(packed, shape):
    body = shape[0] * shape[1]
    code = packed[:body].astype(jnp.float32).reshape(shape)
    expo = packed[body : body + body // shape[2]].astype(jnp.float32).reshape(shape[:2] + (1,))
    tail = packed[-1].astype(jnp.float32)
    decay = (tail[: shape[0]] + tail[shape[0] : 2 * shape[0]] / 16384.0) / 64.0
    return code * jnp.exp2(expo - 15.0), decay


def combine(own, got):
    value = own[0] + jnp.exp(own[1])[:, None, None] * got[0]
    return value, jnp.maximum(own[1] + got[1], FLOOR)


def shift_pair(fwd, bwd, by):
    shape = fwd[0].shape
    fwd, bwd = lax.optimization_barrier((pack(*fwd), pack(*bwd)))
    got_f, got_b = lax.optimization_barrier(
        (from_behind(fwd, "context", by), from_behind(bwd, "context", -by))
    )
    return unpack(got_f, shape), unpack(got_b, shape)


def exchange(pieces, axis):
    count = lax.axis_size(axis)
    pieces = lax.optimization_barrier(pieces)
    got = [
        lax.ppermute(pieces[s], axis, [(i, (i + s) % count) for i in range(count)])
        for s in range(1, count)
    ]
    return [pieces[0]] + list(lax.optimization_barrier(got))


def scatter_sum(whole, axis):
    count = lax.axis_size(axis)
    size = whole.shape[1] // count
    parts = whole.reshape(whole.shape[0], count, size, whole.shape[2]).transpose(1, 0, 2, 3)
    got = lax.all_to_all(parts, axis, 0, 0, tiled=True)
    return jnp.sum(got, axis=0)


def scatter_sum_by_permutes(whole, axis):
    count = lax.axis_size(axis)
    me = lax.axis_index(axis)
    size = whole.shape[1] // count
    pieces = [
        lax.dynamic_slice_in_dim(whole, ((me + s) % count) * size, size, axis=1)
        for s in range(count)
    ]
    got = exchange(pieces, axis)
    out = got[0]
    for part in got[1:]:
        out = out + part
    return out


def local(inputs, grads, step_size, decay_rate, skip_gain, b_rows, c_rows, doc_lengths):
    length = inputs.shape[0]
    heads = step_size.shape[0]
    width = inputs.shape[1] // heads
    count = lax.axis_size("tensor")
    piece = jnp.stack([b_rows, c_rows])
    rows = lax.all_to_all(jnp.broadcast_to(piece, (count,) + piece.shape), "tensor", 0, 0, tiled=True)
    b_bf = rows[:, 0].reshape(length, -1)
    c_bf = rows[:, 1].reshape(length, -1)
    bmat = b_bf.astype(jnp.float32)
    cmat = c_bf.astype(jnp.float32)
    xs = inputs.astype(jnp.float32).reshape(length, heads, width).transpose(1, 0, 2)
    dys = grads.astype(jnp.float32).reshape(length, heads, width).transpose(1, 0, 2)
    offset = lax.axis_index("context") * length
    ends = jnp.cumsum(doc_lengths)
    starts = ends - doc_lengths
    position = offset + jnp.arange(length, dtype=jnp.int32)
    seg = jnp.sum(
        ((starts[None, :] >= offset) & (starts[None, :] <= position[:, None])).astype(jnp.int32),
        axis=1,
    )
    rate = decay_rate[:, None]
    logc = jnp.cumsum(-step_size * rate, axis=1)
    enter = jnp.exp(logc) * (seg == 0).astype(jnp.float32)[None, :]
    leave = jnp.exp(logc[:, -1:] - logc) * (seg == seg[-1]).astype(jnp.float32)[None, :]
    moved = step_size[:, :, None] * xs
    left_u = leave[:, :, None] * moved
    enter_dy = enter[:, :, None] * dys
    local_state = jnp.einsum("hlp,ln->hpn", left_u, bmat, precision=HIGH)
    local_adj = jnp.einsum("hlp,ln->hpn", enter_dy, cmat, precision=HIGH)

    reach = 3 * lax.axis_size("context") // 16
    low = reach & -reach
    high = reach - low
    assert high > 0 and high & (high - 1) == 0 and low < high
    shape = local_state.shape
    decay = jnp.where(seg[-1] == 0, jnp.maximum(logc[:, -1], FLOOR), FLOOR)
    fwd = (local_state, decay)
    bwd = (local_adj, decay)
    span = 1
    kept = {}
    while span < high:
        kept[span] = (fwd, bwd)
        got_f, got_b = shift_pair(fwd, bwd, span)
        fwd = combine(fwd, got_f)
        bwd = combine(bwd, got_b)
        span *= 2
    near_f, near_b = kept[low]
    sends = lax.optimization_barrier((pack(*near_f), pack(*fwd), pack(*near_b), pack(*bwd)))
    got = (
        from_behind(sends[0], "context", 1),
        from_behind(sends[1], "context", low + 1),
        from_behind(sends[2], "context", -1),
        from_behind(sends[3], "context", -low - 1),
    )
    got = [unpack(g, shape) for g in got]
    s_in = combine(got[0], got[1])[0]
    g_in = combine(got[2], got[3])[0]

    index = jnp.arange(length)
    keep = (index[:, None] >= index[None, :]) & (seg[:, None] == seg[None, :])
    weights = jnp.exp(jnp.where(keep[None], logc[:, :, None] - logc[:, None, :], -1e30))
    scores = jnp.dot(c_bf, b_bf.T, preferred_element_type=jnp.float32)
    mixed = weights * scores[None]
    core_loc = jnp.einsum("hij,hip->hjp", mixed, dys, precision=HIGH)
    pairs = jnp.einsum("hip,hjp->hij", dys, moved, precision=HIGH)
    paired = mixed * pairs
    col_total = jnp.sum(paired, axis=1)
    row_total = jnp.sum(paired, axis=2)
    inner = jnp.cumsum(col_total, axis=1) - (jnp.cumsum(row_total, axis=1) - row_total)
    weighted = jnp.sum(weights * pairs, axis=0)
    gb_loc = jnp.dot(weighted.T, cmat, precision=HIGH)
    gc_loc = jnp.dot(weighted, bmat, precision=HIGH)

    b_adj = jnp.einsum("ln,hpn->hlp", bmat, g_in, precision=HIGH)
    c_state = jnp.einsum("ln,hpn->hlp", cmat, s_in, precision=HIGH)
    core = core_loc + leave[:, :, None] * b_adj
    gx = step_size[:, :, None] * core + skip_gain[:, None, None] * dys
    along = jnp.sum(xs * core, axis=2)
    from_state = enter * jnp.einsum(
        "hij,hi->hj", weights, jnp.sum(dys * c_state, axis=2), precision=HIGH
    )
    from_adj = leave * jnp.einsum(
        "hij,hj->hi", weights, jnp.sum(moved * b_adj, axis=2), precision=HIGH
    )
    both = leave * enter * jnp.sum(g_in * s_in, axis=(1, 2))[:, None]
    grad_step = along * (1.0 + rate * step_size) - rate * (inner + from_state + from_adj + both)
    gb = gb_loc + jnp.einsum("hlp,hpn->ln", left_u, g_in, precision=HIGH)
    gc = gc_loc + jnp.einsum("hlp,hpn->ln", enter_dy, s_in, precision=HIGH)

    grad_x = gx.transpose(1, 0, 2).reshape(length, heads * width)
    grad_bc = scatter_sum(jnp.stack([gb, gc]), "tensor")
    return (grad_x, grad_step, grad_bc[0], grad_bc[1])


def solution(mesh):
    in_specs = (
        P("context", "tensor"),
        P("context", "tensor"),
        P("tensor", "context"),
        P("tensor"),
        P("tensor"),
        P(("context", "tensor"), None),
        P(("context", "tensor"), None),
        P(),
    )
    out_specs = (
        P("context", "tensor"),
        P("tensor", "context"),
        P(("context", "tensor"), None),
        P(("context", "tensor"), None),
    )
    return jax.shard_map(local, mesh=mesh, in_specs=in_specs, out_specs=out_specs, check_vma=False)
```

```python
import jax
import jax.numpy as jnp
from jax import lax
from jax.sharding import PartitionSpec as P

HIGH = lax.Precision.HIGHEST


def from_behind(x, axis, by):
    peers = lax.axis_size(axis)
    pairs = [(i, i + by) for i in range(peers) if 0 <= i + by < peers]
    return lax.ppermute(x, axis, pairs)


FLOOR = -150.0


def pack(value, decay):
    top = jnp.max(jnp.abs(value), axis=-1, keepdims=True)
    expo = jnp.maximum(jnp.ceil(jnp.log2(jnp.where(top > 0, top, 1.0))), -100.0)
    code = jnp.clip(jnp.round(value / jnp.exp2(expo - 15.0)), -32767.0, 32767.0).astype(jnp.int16)
    scaled = decay * 64.0
    high = jnp.floor(scaled)
    low = jnp.round((scaled - high) * 16384.0)
    lanes = value.shape[-1]
    tail = jnp.concatenate([high, low, jnp.zeros((lanes - 2 * decay.shape[0],), jnp.float32)])[None]
    return jnp.concatenate(
        [code.reshape(-1, lanes), expo.reshape(-1, lanes).astype(jnp.int16), tail.astype(jnp.int16)]
    )


def unpack(packed, shape):
    body = shape[0] * shape[1]
    code = packed[:body].astype(jnp.float32).reshape(shape)
    expo = packed[body : body + body // shape[2]].astype(jnp.float32).reshape(shape[:2] + (1,))
    tail = packed[-1].astype(jnp.float32)
    decay = (tail[: shape[0]] + tail[shape[0] : 2 * shape[0]] / 16384.0) / 64.0
    return code * jnp.exp2(expo - 15.0), decay


def combine(own, got):
    value = own[0] + jnp.exp(own[1])[:, None, None] * got[0]
    return value, jnp.maximum(own[1] + got[1], FLOOR)


def shift_pair(fwd, bwd, by):
    shape = fwd[0].shape
    fwd, bwd = lax.optimization_barrier((pack(*fwd), pack(*bwd)))
    got_f, got_b = from_behind(fwd, "context", by), from_behind(bwd, "context", -by)
    return unpack(got_f, shape), unpack(got_b, shape)


def exchange(pieces, axis):
    count = lax.axis_size(axis)
    pieces = lax.optimization_barrier(pieces)
    got = [
        lax.ppermute(pieces[s], axis, [(i, (i + s) % count) for i in range(count)])
        for s in range(1, count)
    ]
    return [pieces[0]] + list(lax.optimization_barrier(got))


def scatter_sum(whole, axis):
    count = lax.axis_size(axis)
    size = whole.shape[1] // count
    parts = whole.reshape(whole.shape[0], count, size, whole.shape[2]).transpose(1, 0, 2, 3)
    got = lax.all_to_all(parts, axis, 0, 0, tiled=True)
    return jnp.sum(got, axis=0)


def scatter_sum_by_permutes(whole, axis):
    count = lax.axis_size(axis)
    me = lax.axis_index(axis)
    size = whole.shape[1] // count
    pieces = [
        lax.dynamic_slice_in_dim(whole, ((me + s) % count) * size, size, axis=1)
        for s in range(count)
    ]
    got = exchange(pieces, axis)
    out = got[0]
    for part in got[1:]:
        out = out + part
    return out


def local(inputs, grads, step_size, decay_rate, skip_gain, b_rows, c_rows, doc_lengths):
    length = inputs.shape[0]
    heads = step_size.shape[0]
    width = inputs.shape[1] // heads
    count = lax.axis_size("tensor")
    piece = jnp.stack([b_rows, c_rows])
    rows = lax.all_to_all(jnp.broadcast_to(piece, (count,) + piece.shape), "tensor", 0, 0, tiled=True)
    b_bf = rows[:, 0].reshape(length, -1)
    c_bf = rows[:, 1].reshape(length, -1)
    bmat = b_bf.astype(jnp.float32)
    cmat = c_bf.astype(jnp.float32)
    xs = inputs.astype(jnp.float32).reshape(length, heads, width).transpose(1, 0, 2)
    dys = grads.astype(jnp.float32).reshape(length, heads, width).transpose(1, 0, 2)
    offset = lax.axis_index("context") * length
    ends = jnp.cumsum(doc_lengths)
    starts = ends - doc_lengths
    position = offset + jnp.arange(length, dtype=jnp.int32)
    seg = jnp.sum(
        ((starts[None, :] >= offset) & (starts[None, :] <= position[:, None])).astype(jnp.int32),
        axis=1,
    )
    rate = decay_rate[:, None]
    logc = jnp.cumsum(-step_size * rate, axis=1)
    enter = jnp.exp(logc) * (seg == 0).astype(jnp.float32)[None, :]
    leave = jnp.exp(logc[:, -1:] - logc) * (seg == seg[-1]).astype(jnp.float32)[None, :]
    moved = step_size[:, :, None] * xs
    left_u = leave[:, :, None] * moved
    enter_dy = enter[:, :, None] * dys
    local_state = jnp.einsum("hlp,ln->hpn", left_u, bmat, precision=HIGH)
    local_adj = jnp.einsum("hlp,ln->hpn", enter_dy, cmat, precision=HIGH)

    reach = 3 * lax.axis_size("context") // 16
    low = reach & -reach
    high = reach - low
    assert high > 0 and high & (high - 1) == 0 and low < high
    shape = local_state.shape
    decay = jnp.where(seg[-1] == 0, jnp.maximum(logc[:, -1], FLOOR), FLOOR)
    fwd = (local_state, decay)
    bwd = (local_adj, decay)
    span = 1
    kept = {}
    while span < high:
        kept[span] = (fwd, bwd)
        got_f, got_b = shift_pair(fwd, bwd, span)
        fwd = combine(fwd, got_f)
        bwd = combine(bwd, got_b)
        span *= 2
    near_f, near_b = kept[low]
    sends = lax.optimization_barrier((pack(*near_f), pack(*fwd), pack(*near_b), pack(*bwd)))
    got = (
        from_behind(sends[0], "context", 1),
        from_behind(sends[1], "context", low + 1),
        from_behind(sends[2], "context", -1),
        from_behind(sends[3], "context", -low - 1),
    )
    got = [unpack(g, shape) for g in got]
    s_in = combine(got[0], got[1])[0]
    g_in = combine(got[2], got[3])[0]

    index = jnp.arange(length)
    keep = (index[:, None] >= index[None, :]) & (seg[:, None] == seg[None, :])
    weights = jnp.exp(jnp.where(keep[None], logc[:, :, None] - logc[:, None, :], -1e30))
    scores = jnp.dot(c_bf, b_bf.T, preferred_element_type=jnp.float32)
    mixed = weights * scores[None]
    core_loc = jnp.einsum("hij,hip->hjp", mixed, dys, precision=HIGH)
    pairs = jnp.einsum("hip,hjp->hij", dys, moved, precision=HIGH)
    paired = mixed * pairs
    col_total = jnp.sum(paired, axis=1)
    row_total = jnp.sum(paired, axis=2)
    inner = jnp.cumsum(col_total, axis=1) - (jnp.cumsum(row_total, axis=1) - row_total)
    weighted = jnp.sum(weights * pairs, axis=0)
    gb_loc = jnp.dot(weighted.T, cmat, precision=HIGH)
    gc_loc = jnp.dot(weighted, bmat, precision=HIGH)

    b_adj = jnp.einsum("ln,hpn->hlp", bmat, g_in, precision=HIGH)
    c_state = jnp.einsum("ln,hpn->hlp", cmat, s_in, precision=HIGH)
    core = core_loc + leave[:, :, None] * b_adj
    gx = step_size[:, :, None] * core + skip_gain[:, None, None] * dys
    along = jnp.sum(xs * core, axis=2)
    from_state = enter * jnp.einsum(
        "hij,hi->hj", weights, jnp.sum(dys * c_state, axis=2), precision=HIGH
    )
    from_adj = leave * jnp.einsum(
        "hij,hj->hi", weights, jnp.sum(moved * b_adj, axis=2), precision=HIGH
    )
    both = leave * enter * jnp.sum(g_in * s_in, axis=(1, 2))[:, None]
    grad_step = along * (1.0 + rate * step_size) - rate * (inner + from_state + from_adj + both)
    gb = gb_loc + jnp.einsum("hlp,hpn->ln", left_u, g_in, precision=HIGH)
    gc = gc_loc + jnp.einsum("hlp,hpn->ln", enter_dy, s_in, precision=HIGH)

    grad_x = gx.transpose(1, 0, 2).reshape(length, heads * width)
    grad_bc = scatter_sum(jnp.stack([gb, gc]), "tensor")
    return (grad_x, grad_step, grad_bc[0], grad_bc[1])


def solution(mesh):
    in_specs = (
        P("context", "tensor"),
        P("context", "tensor"),
        P("tensor", "context"),
        P("tensor"),
        P("tensor"),
        P(("context", "tensor"), None),
        P(("context", "tensor"), None),
        P(),
    )
    out_specs = (
        P("context", "tensor"),
        P("tensor", "context"),
        P(("context", "tensor"), None),
        P(("context", "tensor"), None),
    )
    return jax.shard_map(local, mesh=mesh, in_specs=in_specs, out_specs=out_specs, check_vma=False)
```

```python
import jax
import jax.numpy as jnp
from jax import lax
from jax.sharding import PartitionSpec as P

HIGH = lax.Precision.HIGHEST


def from_behind(x, axis, by):
    peers = lax.axis_size(axis)
    pairs = [(i, i + by) for i in range(peers) if 0 <= i + by < peers]
    return lax.ppermute(x, axis, pairs)


FLOOR = -150.0


def pack(value, decay):
    top = jnp.max(jnp.abs(value), axis=-1, keepdims=True)
    expo = jnp.maximum(jnp.ceil(jnp.log2(jnp.where(top > 0, top, 1.0))), -100.0)
    code = jnp.clip(jnp.round(value / jnp.exp2(expo - 15.0)), -32767.0, 32767.0).astype(jnp.int16)
    scaled = decay * 64.0
    high = jnp.floor(scaled)
    low = jnp.round((scaled - high) * 16384.0)
    lanes = value.shape[-1]
    tail = jnp.concatenate([high, low, jnp.zeros((lanes - 2 * decay.shape[0],), jnp.float32)])[None]
    return jnp.concatenate(
        [code.reshape(-1, lanes), expo.reshape(-1, lanes).astype(jnp.int16), tail.astype(jnp.int16)]
    )


def unpack(packed, shape):
    body = shape[0] * shape[1]
    code = packed[:body].astype(jnp.float32).reshape(shape)
    expo = packed[body : body + body // shape[2]].astype(jnp.float32).reshape(shape[:2] + (1,))
    tail = packed[-1].astype(jnp.float32)
    decay = (tail[: shape[0]] + tail[shape[0] : 2 * shape[0]] / 16384.0) / 64.0
    return code * jnp.exp2(expo - 15.0), decay


def combine(own, got):
    value = own[0] + jnp.exp(own[1])[:, None, None] * got[0]
    return value, jnp.maximum(own[1] + got[1], FLOOR)


def shift_pair(fwd, bwd, by):
    shape = fwd[0].shape
    fwd, bwd = lax.optimization_barrier((pack(*fwd), pack(*bwd)))
    got_f, got_b = from_behind(fwd, "context", by), from_behind(bwd, "context", -by)
    return unpack(got_f, shape), unpack(got_b, shape)


def exchange(pieces, axis):
    count = lax.axis_size(axis)
    pieces = lax.optimization_barrier(pieces)
    got = [
        lax.ppermute(pieces[s], axis, [(i, (i + s) % count) for i in range(count)])
        for s in range(1, count)
    ]
    return [pieces[0]] + list(lax.optimization_barrier(got))


def scatter_sum(whole, axis):
    count = lax.axis_size(axis)
    size = whole.shape[1] // count
    parts = whole.reshape(whole.shape[0], count, size, whole.shape[2]).transpose(1, 0, 2, 3)
    got = lax.all_to_all(parts, axis, 0, 0, tiled=True)
    return jnp.sum(got, axis=0)


def scatter_sum_by_permutes(whole, axis):
    count = lax.axis_size(axis)
    me = lax.axis_index(axis)
    size = whole.shape[1] // count
    pieces = [
        lax.dynamic_slice_in_dim(whole, ((me + s) % count) * size, size, axis=1)
        for s in range(count)
    ]
    got = exchange(pieces, axis)
    out = got[0]
    for part in got[1:]:
        out = out + part
    return out


def local(inputs, grads, step_size, decay_rate, skip_gain, b_rows, c_rows, doc_lengths):
    length = inputs.shape[0]
    heads = step_size.shape[0]
    width = inputs.shape[1] // heads
    count = lax.axis_size("tensor")
    piece = jnp.stack([b_rows, c_rows])
    rows = lax.all_to_all(jnp.broadcast_to(piece, (count,) + piece.shape), "tensor", 0, 0, tiled=True)
    b_bf = rows[:, 0].reshape(length, -1)
    c_bf = rows[:, 1].reshape(length, -1)
    bmat = b_bf.astype(jnp.float32)
    cmat = c_bf.astype(jnp.float32)
    xs = inputs.astype(jnp.float32).reshape(length, heads, width).transpose(1, 0, 2)
    dys = grads.astype(jnp.float32).reshape(length, heads, width).transpose(1, 0, 2)
    offset = lax.axis_index("context") * length
    ends = jnp.cumsum(doc_lengths)
    starts = ends - doc_lengths
    position = offset + jnp.arange(length, dtype=jnp.int32)
    seg = jnp.sum(
        ((starts[None, :] >= offset) & (starts[None, :] <= position[:, None])).astype(jnp.int32),
        axis=1,
    )
    rate = decay_rate[:, None]
    logc = jnp.cumsum(-step_size * rate, axis=1)
    enter = jnp.exp(logc) * (seg == 0).astype(jnp.float32)[None, :]
    leave = jnp.exp(logc[:, -1:] - logc) * (seg == seg[-1]).astype(jnp.float32)[None, :]
    moved = step_size[:, :, None] * xs
    left_u = leave[:, :, None] * moved
    enter_dy = enter[:, :, None] * dys
    local_state = jnp.einsum("hlp,ln->hpn", left_u, bmat, precision=HIGH)
    local_adj = jnp.einsum("hlp,ln->hpn", enter_dy, cmat, precision=HIGH)

    index = jnp.arange(length)
    keep = (index[:, None] >= index[None, :]) & (seg[:, None] == seg[None, :])
    weights = jnp.exp(jnp.where(keep[None], logc[:, :, None] - logc[:, None, :], -1e30))
    scores = jnp.dot(c_bf, b_bf.T, preferred_element_type=jnp.float32)
    mixed = weights * scores[None]
    core_loc = jnp.einsum("hij,hip->hjp", mixed, dys, precision=HIGH)
    pairs = jnp.einsum("hip,hjp->hij", dys, moved, precision=HIGH)
    paired = mixed * pairs
    col_total = jnp.sum(paired, axis=1)
    row_total = jnp.sum(paired, axis=2)
    inner = jnp.cumsum(col_total, axis=1) - (jnp.cumsum(row_total, axis=1) - row_total)
    weighted = jnp.sum(weights * pairs, axis=0)
    gb_loc = jnp.dot(weighted.T, cmat, precision=HIGH)
    gc_loc = jnp.dot(weighted, bmat, precision=HIGH)

    local_state, local_adj, weights, core_loc, inner, gb_loc, gc_loc = lax.optimization_barrier(
        (local_state, local_adj, weights, core_loc, inner, gb_loc, gc_loc)
    )

    reach = 3 * lax.axis_size("context") // 16
    low = reach & -reach
    high = reach - low
    assert high > 0 and high & (high - 1) == 0 and low < high
    shape = local_state.shape
    decay = jnp.where(seg[-1] == 0, jnp.maximum(logc[:, -1], FLOOR), FLOOR)
    fwd = (local_state, decay)
    bwd = (local_adj, decay)
    span = 1
    kept = {}
    while span < high:
        kept[span] = (fwd, bwd)
        got_f, got_b = shift_pair(fwd, bwd, span)
        fwd = combine(fwd, got_f)
        bwd = combine(bwd, got_b)
        span *= 2
    near_f, near_b = kept[low]
    sends = lax.optimization_barrier((pack(*near_f), pack(*fwd), pack(*near_b), pack(*bwd)))
    got = (
        from_behind(sends[0], "context", 1),
        from_behind(sends[1], "context", low + 1),
        from_behind(sends[2], "context", -1),
        from_behind(sends[3], "context", -low - 1),
    )
    got = [unpack(g, shape) for g in got]
    s_in = combine(got[0], got[1])[0]
    g_in = combine(got[2], got[3])[0]

    b_adj = jnp.einsum("ln,hpn->hlp", bmat, g_in, precision=HIGH)
    c_state = jnp.einsum("ln,hpn->hlp", cmat, s_in, precision=HIGH)
    core = core_loc + leave[:, :, None] * b_adj
    gx = step_size[:, :, None] * core + skip_gain[:, None, None] * dys
    along = jnp.sum(xs * core, axis=2)
    from_state = enter * jnp.einsum(
        "hij,hi->hj", weights, jnp.sum(dys * c_state, axis=2), precision=HIGH
    )
    from_adj = leave * jnp.einsum(
        "hij,hj->hi", weights, jnp.sum(moved * b_adj, axis=2), precision=HIGH
    )
    both = leave * enter * jnp.sum(g_in * s_in, axis=(1, 2))[:, None]
    grad_step = along * (1.0 + rate * step_size) - rate * (inner + from_state + from_adj + both)
    gb = gb_loc + jnp.einsum("hlp,hpn->ln", left_u, g_in, precision=HIGH)
    gc = gc_loc + jnp.einsum("hlp,hpn->ln", enter_dy, s_in, precision=HIGH)

    grad_x = gx.transpose(1, 0, 2).reshape(length, heads * width)
    grad_bc = scatter_sum(jnp.stack([gb, gc]), "tensor")
    return (grad_x, grad_step, grad_bc[0], grad_bc[1])


def solution(mesh):
    in_specs = (
        P("context", "tensor"),
        P("context", "tensor"),
        P("tensor", "context"),
        P("tensor"),
        P("tensor"),
        P(("context", "tensor"), None),
        P(("context", "tensor"), None),
        P(),
    )
    out_specs = (
        P("context", "tensor"),
        P("tensor", "context"),
        P(("context", "tensor"), None),
        P(("context", "tensor"), None),
    )
    return jax.shard_map(local, mesh=mesh, in_specs=in_specs, out_specs=out_specs, check_vma=False)
```

```python
import jax
import jax.numpy as jnp
from jax import lax
from jax.sharding import PartitionSpec as P

HIGH = lax.Precision.HIGHEST


def from_behind(x, axis, by):
    peers = lax.axis_size(axis)
    pairs = [(i, i + by) for i in range(peers) if 0 <= i + by < peers]
    return lax.ppermute(x, axis, pairs)


FLOOR = -150.0


def pack(value, decay):
    top = jnp.max(jnp.abs(value), axis=-1, keepdims=True)
    expo = jnp.maximum(jnp.ceil(jnp.log2(jnp.where(top > 0, top, 1.0))), -100.0)
    code = jnp.clip(jnp.round(value / jnp.exp2(expo - 15.0)), -32767.0, 32767.0).astype(jnp.int16)
    scaled = decay * 64.0
    high = jnp.floor(scaled)
    low = jnp.round((scaled - high) * 16384.0)
    lanes = value.shape[-1]
    tail = jnp.concatenate([high, low, jnp.zeros((lanes - 2 * decay.shape[0],), jnp.float32)])[None]
    return jnp.concatenate(
        [code.reshape(-1, lanes), expo.reshape(-1, lanes).astype(jnp.int16), tail.astype(jnp.int16)]
    )


def unpack(packed, shape):
    body = shape[0] * shape[1]
    code = packed[:body].astype(jnp.float32).reshape(shape)
    expo = packed[body : body + body // shape[2]].astype(jnp.float32).reshape(shape[:2] + (1,))
    tail = packed[-1].astype(jnp.float32)
    decay = (tail[: shape[0]] + tail[shape[0] : 2 * shape[0]] / 16384.0) / 64.0
    return code * jnp.exp2(expo - 15.0), decay


def combine(own, got):
    value = own[0] + jnp.exp(own[1])[:, None, None] * got[0]
    return value, jnp.maximum(own[1] + got[1], FLOOR)


def shift_pair(fwd, bwd, by, held=()):
    shape = fwd[0].shape
    fwd, bwd, held = lax.optimization_barrier((pack(*fwd), pack(*bwd), held))
    got_f, got_b = from_behind(fwd, "context", by), from_behind(bwd, "context", -by)
    return unpack(got_f, shape), unpack(got_b, shape), held


def exchange(pieces, axis):
    count = lax.axis_size(axis)
    pieces = lax.optimization_barrier(pieces)
    got = [
        lax.ppermute(pieces[s], axis, [(i, (i + s) % count) for i in range(count)])
        for s in range(1, count)
    ]
    return [pieces[0]] + list(lax.optimization_barrier(got))


def scatter_sum(whole, axis):
    count = lax.axis_size(axis)
    size = whole.shape[1] // count
    parts = whole.reshape(whole.shape[0], count, size, whole.shape[2]).transpose(1, 0, 2, 3)
    got = lax.all_to_all(parts, axis, 0, 0, tiled=True)
    return jnp.sum(got, axis=0)


def scatter_sum_by_permutes(whole, axis):
    count = lax.axis_size(axis)
    me = lax.axis_index(axis)
    size = whole.shape[1] // count
    pieces = [
        lax.dynamic_slice_in_dim(whole, ((me + s) % count) * size, size, axis=1)
        for s in range(count)
    ]
    got = exchange(pieces, axis)
    out = got[0]
    for part in got[1:]:
        out = out + part
    return out


def local(inputs, grads, step_size, decay_rate, skip_gain, b_rows, c_rows, doc_lengths):
    length = inputs.shape[0]
    heads = step_size.shape[0]
    width = inputs.shape[1] // heads
    count = lax.axis_size("tensor")
    piece = jnp.stack([b_rows, c_rows])
    rows = lax.all_to_all(jnp.broadcast_to(piece, (count,) + piece.shape), "tensor", 0, 0, tiled=True)
    b_bf = rows[:, 0].reshape(length, -1)
    c_bf = rows[:, 1].reshape(length, -1)
    bmat = b_bf.astype(jnp.float32)
    cmat = c_bf.astype(jnp.float32)
    xs = inputs.astype(jnp.float32).reshape(length, heads, width).transpose(1, 0, 2)
    dys = grads.astype(jnp.float32).reshape(length, heads, width).transpose(1, 0, 2)
    offset = lax.axis_index("context") * length
    ends = jnp.cumsum(doc_lengths)
    starts = ends - doc_lengths
    position = offset + jnp.arange(length, dtype=jnp.int32)
    seg = jnp.sum(
        ((starts[None, :] >= offset) & (starts[None, :] <= position[:, None])).astype(jnp.int32),
        axis=1,
    )
    rate = decay_rate[:, None]
    logc = jnp.cumsum(-step_size * rate, axis=1)
    enter = jnp.exp(logc) * (seg == 0).astype(jnp.float32)[None, :]
    leave = jnp.exp(logc[:, -1:] - logc) * (seg == seg[-1]).astype(jnp.float32)[None, :]
    moved = step_size[:, :, None] * xs
    left_u = leave[:, :, None] * moved
    enter_dy = enter[:, :, None] * dys
    local_state = jnp.einsum("hlp,ln->hpn", left_u, bmat, precision=HIGH)
    local_adj = jnp.einsum("hlp,ln->hpn", enter_dy, cmat, precision=HIGH)

    reach = 3 * lax.axis_size("context") // 16
    low = reach & -reach
    high = reach - low
    assert high > 0 and high & (high - 1) == 0 and low < high
    shape = local_state.shape
    decay = jnp.where(seg[-1] == 0, jnp.maximum(logc[:, -1], FLOOR), FLOOR)
    fwd = (local_state, decay)
    bwd = (local_adj, decay)
    span = 1
    kept = {}
    held = (logc, dys, moved, b_bf, c_bf)
    while span < high:
        kept[span] = (fwd, bwd)
        if 2 * span < high:
            got_f, got_b, _ = shift_pair(fwd, bwd, span)
        else:
            got_f, got_b, held = shift_pair(fwd, bwd, span, held)
        fwd = combine(fwd, got_f)
        bwd = combine(bwd, got_b)
        span *= 2
    near_f, near_b = kept[low]
    sends = lax.optimization_barrier((pack(*near_f), pack(*fwd), pack(*near_b), pack(*bwd)))
    got = (
        from_behind(sends[0], "context", 1),
        from_behind(sends[1], "context", low + 1),
        from_behind(sends[2], "context", -1),
        from_behind(sends[3], "context", -low - 1),
    )
    got = [unpack(g, shape) for g in got]
    s_in = combine(got[0], got[1])[0]
    g_in = combine(got[2], got[3])[0]

    late_logc, late_dys, late_moved, late_b, late_c = held
    index = jnp.arange(length)
    keep = (index[:, None] >= index[None, :]) & (seg[:, None] == seg[None, :])
    weights = jnp.exp(
        jnp.where(keep[None], late_logc[:, :, None] - late_logc[:, None, :], -1e30)
    )
    scores = jnp.dot(late_c, late_b.T, preferred_element_type=jnp.float32)
    mixed = weights * scores[None]
    core_loc = jnp.einsum("hij,hip->hjp", mixed, late_dys, precision=HIGH)
    pairs = jnp.einsum("hip,hjp->hij", late_dys, late_moved, precision=HIGH)
    paired = mixed * pairs
    col_total = jnp.sum(paired, axis=1)
    row_total = jnp.sum(paired, axis=2)
    inner = jnp.cumsum(col_total, axis=1) - (jnp.cumsum(row_total, axis=1) - row_total)
    weighted = jnp.sum(weights * pairs, axis=0)
    gb_loc = jnp.dot(weighted.T, cmat, precision=HIGH)
    gc_loc = jnp.dot(weighted, bmat, precision=HIGH)

    b_adj = jnp.einsum("ln,hpn->hlp", bmat, g_in, precision=HIGH)
    c_state = jnp.einsum("ln,hpn->hlp", cmat, s_in, precision=HIGH)
    core = core_loc + leave[:, :, None] * b_adj
    gx = step_size[:, :, None] * core + skip_gain[:, None, None] * dys
    along = jnp.sum(xs * core, axis=2)
    from_state = enter * jnp.einsum(
        "hij,hi->hj", weights, jnp.sum(dys * c_state, axis=2), precision=HIGH
    )
    from_adj = leave * jnp.einsum(
        "hij,hj->hi", weights, jnp.sum(moved * b_adj, axis=2), precision=HIGH
    )
    both = leave * enter * jnp.sum(g_in * s_in, axis=(1, 2))[:, None]
    grad_step = along * (1.0 + rate * step_size) - rate * (inner + from_state + from_adj + both)
    gb = gb_loc + jnp.einsum("hlp,hpn->ln", left_u, g_in, precision=HIGH)
    gc = gc_loc + jnp.einsum("hlp,hpn->ln", enter_dy, s_in, precision=HIGH)

    grad_x = gx.transpose(1, 0, 2).reshape(length, heads * width)
    grad_bc = scatter_sum(jnp.stack([gb, gc]), "tensor")
    return (grad_x, grad_step, grad_bc[0], grad_bc[1])


def solution(mesh):
    in_specs = (
        P("context", "tensor"),
        P("context", "tensor"),
        P("tensor", "context"),
        P("tensor"),
        P("tensor"),
        P(("context", "tensor"), None),
        P(("context", "tensor"), None),
        P(),
    )
    out_specs = (
        P("context", "tensor"),
        P("tensor", "context"),
        P(("context", "tensor"), None),
        P(("context", "tensor"), None),
    )
    return jax.shard_map(local, mesh=mesh, in_specs=in_specs, out_specs=out_specs, check_vma=False)
```

```python
import jax
import jax.numpy as jnp
from jax import lax
from jax.sharding import PartitionSpec as P

HIGH = lax.Precision.HIGHEST


def from_behind(x, axis, by):
    peers = lax.axis_size(axis)
    pairs = [(i, i + by) for i in range(peers) if 0 <= i + by < peers]
    return lax.ppermute(x, axis, pairs)


FLOOR = -150.0


def pack(value, decay):
    top = jnp.max(jnp.abs(value), axis=-1, keepdims=True)
    expo = jnp.maximum(jnp.ceil(jnp.log2(jnp.where(top > 0, top, 1.0))), -100.0)
    code = jnp.clip(jnp.round(value / jnp.exp2(expo - 15.0)), -32767.0, 32767.0).astype(jnp.int16)
    scaled = decay * 64.0
    high = jnp.floor(scaled)
    low = jnp.round((scaled - high) * 16384.0)
    lanes = value.shape[-1]
    tail = jnp.concatenate([high, low, jnp.zeros((lanes - 2 * decay.shape[0],), jnp.float32)])[None]
    return jnp.concatenate(
        [code.reshape(-1, lanes), expo.reshape(-1, lanes).astype(jnp.int16), tail.astype(jnp.int16)]
    )


def unpack(packed, shape):
    body = shape[0] * shape[1]
    code = packed[:body].astype(jnp.float32).reshape(shape)
    expo = packed[body : body + body // shape[2]].astype(jnp.float32).reshape(shape[:2] + (1,))
    tail = packed[-1].astype(jnp.float32)
    decay = (tail[: shape[0]] + tail[shape[0] : 2 * shape[0]] / 16384.0) / 64.0
    return code * jnp.exp2(expo - 15.0), decay


def combine(own, got):
    value = own[0] + jnp.exp(own[1])[:, None, None] * got[0]
    return value, jnp.maximum(own[1] + got[1], FLOOR)


def shift_pair(fwd, bwd, by, held=()):
    shape = fwd[0].shape
    fwd, bwd, held = lax.optimization_barrier((pack(*fwd), pack(*bwd), held))
    got_f, got_b = from_behind(fwd, "context", by), from_behind(bwd, "context", -by)
    return unpack(got_f, shape), unpack(got_b, shape), held


def exchange(pieces, axis):
    count = lax.axis_size(axis)
    pieces = lax.optimization_barrier(pieces)
    got = [
        lax.ppermute(pieces[s], axis, [(i, (i + s) % count) for i in range(count)])
        for s in range(1, count)
    ]
    return [pieces[0]] + list(lax.optimization_barrier(got))


def scatter_sum(whole, axis):
    count = lax.axis_size(axis)
    size = whole.shape[1] // count
    parts = whole.reshape(whole.shape[0], count, size, whole.shape[2]).transpose(1, 0, 2, 3)
    got = lax.all_to_all(parts, axis, 0, 0, tiled=True)
    return jnp.sum(got, axis=0)


def scatter_sum_by_permutes(whole, axis):
    count = lax.axis_size(axis)
    me = lax.axis_index(axis)
    size = whole.shape[1] // count
    pieces = [
        lax.dynamic_slice_in_dim(whole, ((me + s) % count) * size, size, axis=1)
        for s in range(count)
    ]
    got = exchange(pieces, axis)
    out = got[0]
    for part in got[1:]:
        out = out + part
    return out


def local(inputs, grads, step_size, decay_rate, skip_gain, b_rows, c_rows, doc_lengths):
    length = inputs.shape[0]
    heads = step_size.shape[0]
    width = inputs.shape[1] // heads
    count = lax.axis_size("tensor")
    piece = jnp.stack([b_rows, c_rows])
    rows = lax.all_to_all(jnp.broadcast_to(piece, (count,) + piece.shape), "tensor", 0, 0, tiled=True)
    b_bf = rows[:, 0].reshape(length, -1)
    c_bf = rows[:, 1].reshape(length, -1)
    bmat = b_bf.astype(jnp.float32)
    cmat = c_bf.astype(jnp.float32)
    xs = inputs.astype(jnp.float32).reshape(length, heads, width).transpose(1, 0, 2)
    dys = grads.astype(jnp.float32).reshape(length, heads, width).transpose(1, 0, 2)
    offset = lax.axis_index("context") * length
    ends = jnp.cumsum(doc_lengths)
    starts = ends - doc_lengths
    position = offset + jnp.arange(length, dtype=jnp.int32)
    seg = jnp.sum(
        ((starts[None, :] >= offset) & (starts[None, :] <= position[:, None])).astype(jnp.int32),
        axis=1,
    )
    rate = decay_rate[:, None]
    logc = jnp.cumsum(-step_size * rate, axis=1)
    enter = jnp.exp(logc) * (seg == 0).astype(jnp.float32)[None, :]
    leave = jnp.exp(logc[:, -1:] - logc) * (seg == seg[-1]).astype(jnp.float32)[None, :]
    moved = step_size[:, :, None] * xs
    left_u = leave[:, :, None] * moved
    enter_dy = enter[:, :, None] * dys
    local_state = jnp.einsum("hlp,ln->hpn", left_u, bmat, precision=HIGH)
    local_adj = jnp.einsum("hlp,ln->hpn", enter_dy, cmat, precision=HIGH)

    reach = 3 * lax.axis_size("context") // 16
    low = reach & -reach
    high = reach - low
    assert high > 0 and high & (high - 1) == 0 and low < high
    shape = local_state.shape
    decay = jnp.where(seg[-1] == 0, jnp.maximum(logc[:, -1], FLOOR), FLOOR)
    fwd = (local_state, decay)
    bwd = (local_adj, decay)
    span = 1
    kept = {}
    held = (logc, dys, moved, b_bf, c_bf)
    while span < high:
        kept[span] = (fwd, bwd)
        if 2 * span < high:
            got_f, got_b, _ = shift_pair(fwd, bwd, span)
        else:
            got_f, got_b, held = shift_pair(fwd, bwd, span, held)
        fwd = combine(fwd, got_f)
        bwd = combine(bwd, got_b)
        span *= 2
    near_f, near_b = kept[low]
    sends = lax.optimization_barrier((pack(*near_f), pack(*fwd), pack(*near_b), pack(*bwd)))
    got = (
        from_behind(sends[0], "context", 1),
        from_behind(sends[1], "context", low + 1),
        from_behind(sends[2], "context", -1),
        from_behind(sends[3], "context", -low - 1),
    )
    got = [unpack(g, shape) for g in got]
    s_in = combine(got[0], got[1])[0]
    g_in = combine(got[2], got[3])[0]

    late_logc, late_dys, late_moved, late_b, late_c = held
    index = jnp.arange(length)
    keep = (index[:, None] >= index[None, :]) & (seg[:, None] == seg[None, :])
    weights = jnp.exp(
        jnp.where(keep[None], late_logc[:, :, None] - late_logc[:, None, :], -1e30)
    )
    scores = jnp.dot(late_c, late_b.T, preferred_element_type=jnp.float32)
    mixed = weights * scores[None]
    core_loc = jnp.einsum("hij,hip->hjp", mixed, late_dys, precision=HIGH)
    pairs = jnp.einsum("hip,hjp->hij", late_dys, late_moved, precision=HIGH)
    paired = mixed * pairs
    col_total = jnp.sum(paired, axis=1)
    row_total = jnp.sum(paired, axis=2)
    inner = jnp.cumsum(col_total, axis=1) - (jnp.cumsum(row_total, axis=1) - row_total)
    weighted = jnp.sum(weights * pairs, axis=0)
    gb_loc = jnp.dot(weighted.T, cmat, precision=HIGH)
    gc_loc = jnp.dot(weighted, bmat, precision=HIGH)

    gb = gb_loc + jnp.einsum("hlp,hpn->ln", left_u, g_in, precision=HIGH)
    gc = gc_loc + jnp.einsum("hlp,hpn->ln", enter_dy, s_in, precision=HIGH)
    sums = jnp.stack([gb, gc])
    grad_bc = scatter_sum(sums, "tensor")
    _, b_adj, c_state = lax.optimization_barrier(
        (
            sums,
            jnp.einsum("ln,hpn->hlp", bmat, g_in, precision=HIGH),
            jnp.einsum("ln,hpn->hlp", cmat, s_in, precision=HIGH),
        )
    )
    core = core_loc + leave[:, :, None] * b_adj
    gx = step_size[:, :, None] * core + skip_gain[:, None, None] * dys
    along = jnp.sum(xs * core, axis=2)
    from_state = enter * jnp.einsum(
        "hij,hi->hj", weights, jnp.sum(dys * c_state, axis=2), precision=HIGH
    )
    from_adj = leave * jnp.einsum(
        "hij,hj->hi", weights, jnp.sum(moved * b_adj, axis=2), precision=HIGH
    )
    both = leave * enter * jnp.sum(g_in * s_in, axis=(1, 2))[:, None]
    grad_step = along * (1.0 + rate * step_size) - rate * (inner + from_state + from_adj + both)

    grad_x = gx.transpose(1, 0, 2).reshape(length, heads * width)
    return (grad_x, grad_step, grad_bc[0], grad_bc[1])


def solution(mesh):
    in_specs = (
        P("context", "tensor"),
        P("context", "tensor"),
        P("tensor", "context"),
        P("tensor"),
        P("tensor"),
        P(("context", "tensor"), None),
        P(("context", "tensor"), None),
        P(),
    )
    out_specs = (
        P("context", "tensor"),
        P("tensor", "context"),
        P(("context", "tensor"), None),
        P(("context", "tensor"), None),
    )
    return jax.shard_map(local, mesh=mesh, in_specs=in_specs, out_specs=out_specs, check_vma=False)
```

```python
import jax
import jax.numpy as jnp
from jax import lax
from jax.sharding import PartitionSpec as P

HIGH = lax.Precision.HIGHEST


def from_behind(x, axis, by):
    peers = lax.axis_size(axis)
    pairs = [(i, i + by) for i in range(peers) if 0 <= i + by < peers]
    return lax.ppermute(x, axis, pairs)


FLOOR = -150.0


def pack(value, decay):
    top = jnp.max(jnp.abs(value), axis=-1, keepdims=True)
    expo = jnp.maximum(jnp.ceil(jnp.log2(jnp.where(top > 0, top, 1.0))), -100.0)
    code = jnp.clip(jnp.round(value / jnp.exp2(expo - 15.0)), -32767.0, 32767.0).astype(jnp.int16)
    scaled = decay * 64.0
    high = jnp.floor(scaled)
    low = jnp.round((scaled - high) * 16384.0)
    lanes = value.shape[-1]
    tail = jnp.concatenate([high, low, jnp.zeros((lanes - 2 * decay.shape[0],), jnp.float32)])[None]
    return jnp.concatenate(
        [code.reshape(-1, lanes), expo.reshape(-1, lanes).astype(jnp.int16), tail.astype(jnp.int16)]
    )


def unpack(packed, shape):
    body = shape[0] * shape[1]
    code = packed[:body].astype(jnp.float32).reshape(shape)
    expo = packed[body : body + body // shape[2]].astype(jnp.float32).reshape(shape[:2] + (1,))
    tail = packed[-1].astype(jnp.float32)
    decay = (tail[: shape[0]] + tail[shape[0] : 2 * shape[0]] / 16384.0) / 64.0
    return code * jnp.exp2(expo - 15.0), decay


def combine(own, got):
    value = own[0] + jnp.exp(own[1])[:, None, None] * got[0]
    return value, jnp.maximum(own[1] + got[1], FLOOR)


def shift_pair(fwd, bwd, by, held=()):
    shape = fwd[0].shape
    fwd, bwd, held = lax.optimization_barrier((pack(*fwd), pack(*bwd), held))
    got_f, got_b = from_behind(fwd, "context", by), from_behind(bwd, "context", -by)
    return unpack(got_f, shape), unpack(got_b, shape), held


def exchange(pieces, axis):
    count = lax.axis_size(axis)
    pieces = lax.optimization_barrier(pieces)
    got = [
        lax.ppermute(pieces[s], axis, [(i, (i + s) % count) for i in range(count)])
        for s in range(1, count)
    ]
    return [pieces[0]] + list(lax.optimization_barrier(got))


def scatter_sum(whole, axis):
    count = lax.axis_size(axis)
    size = whole.shape[1] // count
    parts = whole.reshape(whole.shape[0], count, size, whole.shape[2]).transpose(1, 0, 2, 3)
    got = lax.all_to_all(parts, axis, 0, 0, tiled=True)
    return jnp.sum(got, axis=0)


def scatter_sum_by_permutes(whole, axis):
    count = lax.axis_size(axis)
    me = lax.axis_index(axis)
    size = whole.shape[1] // count
    pieces = [
        lax.dynamic_slice_in_dim(whole, ((me + s) % count) * size, size, axis=1)
        for s in range(count)
    ]
    got = exchange(pieces, axis)
    out = got[0]
    for part in got[1:]:
        out = out + part
    return out


def local(inputs, grads, step_size, decay_rate, skip_gain, b_rows, c_rows, doc_lengths):
    length = inputs.shape[0]
    heads = step_size.shape[0]
    width = inputs.shape[1] // heads
    count = lax.axis_size("tensor")
    piece = jnp.stack([b_rows, c_rows])
    rows = lax.all_to_all(jnp.broadcast_to(piece, (count,) + piece.shape), "tensor", 0, 0, tiled=True)
    b_bf = rows[:, 0].reshape(length, -1)
    c_bf = rows[:, 1].reshape(length, -1)
    bmat = b_bf.astype(jnp.float32)
    cmat = c_bf.astype(jnp.float32)
    xs = inputs.astype(jnp.float32).reshape(length, heads, width).transpose(1, 0, 2)
    dys = grads.astype(jnp.float32).reshape(length, heads, width).transpose(1, 0, 2)
    offset = lax.axis_index("context") * length
    ends = jnp.cumsum(doc_lengths)
    starts = ends - doc_lengths
    position = offset + jnp.arange(length, dtype=jnp.int32)
    seg = jnp.sum(
        ((starts[None, :] >= offset) & (starts[None, :] <= position[:, None])).astype(jnp.int32),
        axis=1,
    )
    rate = decay_rate[:, None]
    logc = jnp.cumsum(-step_size * rate, axis=1)
    enter = jnp.exp(logc) * (seg == 0).astype(jnp.float32)[None, :]
    leave = jnp.exp(logc[:, -1:] - logc) * (seg == seg[-1]).astype(jnp.float32)[None, :]
    moved = step_size[:, :, None] * xs
    left_u = leave[:, :, None] * moved
    enter_dy = enter[:, :, None] * dys
    local_state = jnp.einsum("hlp,ln->hpn", left_u, bmat, precision=HIGH)
    local_adj = jnp.einsum("hlp,ln->hpn", enter_dy, cmat, precision=HIGH)

    reach = 3 * lax.axis_size("context") // 16
    low = reach & -reach
    high = reach - low
    assert high > 0 and high & (high - 1) == 0 and low < high
    shape = local_state.shape
    decay = jnp.where(seg[-1] == 0, jnp.maximum(logc[:, -1], FLOOR), FLOOR)
    fwd = (local_state, decay)
    bwd = (local_adj, decay)
    span = 1
    kept = {}
    held = (logc, dys, moved, b_bf, c_bf)
    while span < high:
        kept[span] = (fwd, bwd)
        got_f, got_b, _ = shift_pair(fwd, bwd, span)
        fwd = combine(fwd, got_f)
        bwd = combine(bwd, got_b)
        span *= 2
    near_f, near_b = kept[low]
    sends = lax.optimization_barrier((pack(*near_f), pack(*fwd), pack(*near_b), pack(*bwd)))
    got = (
        from_behind(sends[0], "context", 1),
        from_behind(sends[1], "context", low + 1),
        from_behind(sends[2], "context", -1),
        from_behind(sends[3], "context", -low - 1),
    )
    first, held = lax.optimization_barrier((got[0], held))
    got = [unpack(g, shape) for g in (first,) + got[1:]]
    s_in = combine(got[0], got[1])[0]
    g_in = combine(got[2], got[3])[0]

    late_logc, late_dys, late_moved, late_b, late_c = held
    index = jnp.arange(length)
    keep = (index[:, None] >= index[None, :]) & (seg[:, None] == seg[None, :])
    weights = jnp.exp(
        jnp.where(keep[None], late_logc[:, :, None] - late_logc[:, None, :], -1e30)
    )
    scores = jnp.dot(late_c, late_b.T, preferred_element_type=jnp.float32)
    mixed = weights * scores[None]
    core_loc = jnp.einsum("hij,hip->hjp", mixed, late_dys, precision=HIGH)
    pairs = jnp.einsum("hip,hjp->hij", late_dys, late_moved, precision=HIGH)
    paired = mixed * pairs
    col_total = jnp.sum(paired, axis=1)
    row_total = jnp.sum(paired, axis=2)
    inner = jnp.cumsum(col_total, axis=1) - (jnp.cumsum(row_total, axis=1) - row_total)
    weighted = jnp.sum(weights * pairs, axis=0)
    gb_loc = jnp.dot(weighted.T, cmat, precision=HIGH)
    gc_loc = jnp.dot(weighted, bmat, precision=HIGH)

    b_adj = jnp.einsum("ln,hpn->hlp", bmat, g_in, precision=HIGH)
    c_state = jnp.einsum("ln,hpn->hlp", cmat, s_in, precision=HIGH)
    core = core_loc + leave[:, :, None] * b_adj
    gx = step_size[:, :, None] * core + skip_gain[:, None, None] * dys
    along = jnp.sum(xs * core, axis=2)
    from_state = enter * jnp.einsum(
        "hij,hi->hj", weights, jnp.sum(dys * c_state, axis=2), precision=HIGH
    )
    from_adj = leave * jnp.einsum(
        "hij,hj->hi", weights, jnp.sum(moved * b_adj, axis=2), precision=HIGH
    )
    both = leave * enter * jnp.sum(g_in * s_in, axis=(1, 2))[:, None]
    grad_step = along * (1.0 + rate * step_size) - rate * (inner + from_state + from_adj + both)
    gb = gb_loc + jnp.einsum("hlp,hpn->ln", left_u, g_in, precision=HIGH)
    gc = gc_loc + jnp.einsum("hlp,hpn->ln", enter_dy, s_in, precision=HIGH)

    grad_x = gx.transpose(1, 0, 2).reshape(length, heads * width)
    grad_bc = scatter_sum(jnp.stack([gb, gc]), "tensor")
    return (grad_x, grad_step, grad_bc[0], grad_bc[1])


def solution(mesh):
    in_specs = (
        P("context", "tensor"),
        P("context", "tensor"),
        P("tensor", "context"),
        P("tensor"),
        P("tensor"),
        P(("context", "tensor"), None),
        P(("context", "tensor"), None),
        P(),
    )
    out_specs = (
        P("context", "tensor"),
        P("tensor", "context"),
        P(("context", "tensor"), None),
        P(("context", "tensor"), None),
    )
    return jax.shard_map(local, mesh=mesh, in_specs=in_specs, out_specs=out_specs, check_vma=False)
```

```python
import jax
import jax.numpy as jnp
from jax import lax
from jax.sharding import PartitionSpec as P

HIGH = lax.Precision.HIGHEST


def from_behind(x, axis, by):
    peers = lax.axis_size(axis)
    pairs = [(i, i + by) for i in range(peers) if 0 <= i + by < peers]
    return lax.ppermute(x, axis, pairs)


FLOOR = -150.0


def pack(value, decay):
    top = jnp.max(jnp.abs(value), axis=-1, keepdims=True)
    expo = jnp.maximum(jnp.ceil(jnp.log2(jnp.where(top > 0, top, 1.0))), -100.0)
    code = jnp.clip(jnp.round(value * jnp.exp2(15.0 - expo)), -32767.0, 32767.0).astype(jnp.int16)
    scaled = decay * 64.0
    high = jnp.floor(scaled)
    low = jnp.round((scaled - high) * 16384.0)
    lanes = value.shape[-1]
    tail = jnp.concatenate([high, low, jnp.zeros((lanes - 2 * decay.shape[0],), jnp.float32)])[None]
    return jnp.concatenate(
        [code.reshape(-1, lanes), expo.reshape(-1, lanes).astype(jnp.int16), tail.astype(jnp.int16)]
    )


def unpack(packed, shape):
    body = shape[0] * shape[1]
    code = packed[:body].astype(jnp.float32).reshape(shape)
    expo = packed[body : body + body // shape[2]].astype(jnp.float32).reshape(shape[:2] + (1,))
    tail = packed[-1].astype(jnp.float32)
    decay = (tail[: shape[0]] + tail[shape[0] : 2 * shape[0]] / 16384.0) / 64.0
    return code * jnp.exp2(expo - 15.0), decay


def combine(own, got):
    value = own[0] + jnp.exp(own[1])[:, None, None] * got[0]
    return value, jnp.maximum(own[1] + got[1], FLOOR)


def shift_pair(fwd, bwd, by, held=()):
    shape = fwd[0].shape
    fwd, bwd, held = lax.optimization_barrier((pack(*fwd), pack(*bwd), held))
    got_f, got_b = from_behind(fwd, "context", by), from_behind(bwd, "context", -by)
    return unpack(got_f, shape), unpack(got_b, shape), held


def exchange(pieces, axis):
    count = lax.axis_size(axis)
    pieces = lax.optimization_barrier(pieces)
    got = [
        lax.ppermute(pieces[s], axis, [(i, (i + s) % count) for i in range(count)])
        for s in range(1, count)
    ]
    return [pieces[0]] + list(lax.optimization_barrier(got))


def scatter_sum(whole, axis):
    count = lax.axis_size(axis)
    size = whole.shape[1] // count
    parts = whole.reshape(whole.shape[0], count, size, whole.shape[2]).transpose(1, 0, 2, 3)
    got = lax.all_to_all(parts, axis, 0, 0, tiled=True)
    return jnp.sum(got, axis=0)


def scatter_sum_by_permutes(whole, axis):
    count = lax.axis_size(axis)
    me = lax.axis_index(axis)
    size = whole.shape[1] // count
    pieces = [
        lax.dynamic_slice_in_dim(whole, ((me + s) % count) * size, size, axis=1)
        for s in range(count)
    ]
    got = exchange(pieces, axis)
    out = got[0]
    for part in got[1:]:
        out = out + part
    return out


def local(inputs, grads, step_size, decay_rate, skip_gain, b_rows, c_rows, doc_lengths):
    length = inputs.shape[0]
    heads = step_size.shape[0]
    width = inputs.shape[1] // heads
    count = lax.axis_size("tensor")
    piece = jnp.stack([b_rows, c_rows])
    rows = lax.all_to_all(jnp.broadcast_to(piece, (count,) + piece.shape), "tensor", 0, 0, tiled=True)
    b_bf = rows[:, 0].reshape(length, -1)
    c_bf = rows[:, 1].reshape(length, -1)
    bmat = b_bf.astype(jnp.float32)
    cmat = c_bf.astype(jnp.float32)
    xs = inputs.astype(jnp.float32).reshape(length, heads, width).transpose(1, 0, 2)
    dys = grads.astype(jnp.float32).reshape(length, heads, width).transpose(1, 0, 2)
    offset = lax.axis_index("context") * length
    ends = jnp.cumsum(doc_lengths)
    starts = ends - doc_lengths
    position = offset + jnp.arange(length, dtype=jnp.int32)
    seg = jnp.sum(
        ((starts[None, :] >= offset) & (starts[None, :] <= position[:, None])).astype(jnp.int32),
        axis=1,
    )
    rate = decay_rate[:, None]
    logc = jnp.cumsum(-step_size * rate, axis=1)
    enter = jnp.exp(logc) * (seg == 0).astype(jnp.float32)[None, :]
    leave = jnp.exp(logc[:, -1:] - logc) * (seg == seg[-1]).astype(jnp.float32)[None, :]
    moved = step_size[:, :, None] * xs
    left_u = leave[:, :, None] * moved
    enter_dy = enter[:, :, None] * dys
    local_state = jnp.einsum("hlp,ln->hpn", left_u, bmat, precision=HIGH)
    local_adj = jnp.einsum("hlp,ln->hpn", enter_dy, cmat, precision=HIGH)

    reach = 3 * lax.axis_size("context") // 16
    low = reach & -reach
    high = reach - low
    assert high > 0 and high & (high - 1) == 0 and low < high
    shape = local_state.shape
    decay = jnp.where(seg[-1] == 0, jnp.maximum(logc[:, -1], FLOOR), FLOOR)
    fwd = (local_state, decay)
    bwd = (local_adj, decay)
    span = 1
    kept = {}
    held = (logc, dys, moved, b_bf, c_bf)
    while span < high:
        kept[span] = (fwd, bwd)
        if 2 * span < high:
            got_f, got_b, _ = shift_pair(fwd, bwd, span)
        else:
            got_f, got_b, held = shift_pair(fwd, bwd, span, held)
        fwd = combine(fwd, got_f)
        bwd = combine(bwd, got_b)
        span *= 2
    near_f, near_b = kept[low]
    sends = lax.optimization_barrier((pack(*near_f), pack(*fwd), pack(*near_b), pack(*bwd)))
    got = (
        from_behind(sends[0], "context", 1),
        from_behind(sends[1], "context", low + 1),
        from_behind(sends[2], "context", -1),
        from_behind(sends[3], "context", -low - 1),
    )
    got = [unpack(g, shape) for g in got]
    s_in = combine(got[0], got[1])[0]
    g_in = combine(got[2], got[3])[0]

    late_logc, late_dys, late_moved, late_b, late_c = held
    index = jnp.arange(length)
    keep = (index[:, None] >= index[None, :]) & (seg[:, None] == seg[None, :])
    weights = jnp.exp(
        jnp.where(keep[None], late_logc[:, :, None] - late_logc[:, None, :], -1e30)
    )
    scores = jnp.dot(late_c, late_b.T, preferred_element_type=jnp.float32)
    mixed = weights * scores[None]
    core_loc = jnp.einsum("hij,hip->hjp", mixed, late_dys, precision=HIGH)
    pairs = jnp.einsum("hip,hjp->hij", late_dys, late_moved, precision=HIGH)
    paired = mixed * pairs
    col_total = jnp.sum(paired, axis=1)
    row_total = jnp.sum(paired, axis=2)
    inner = jnp.cumsum(col_total, axis=1) - (jnp.cumsum(row_total, axis=1) - row_total)
    weighted = jnp.sum(weights * pairs, axis=0)
    gb_loc = jnp.dot(weighted.T, cmat, precision=HIGH)
    gc_loc = jnp.dot(weighted, bmat, precision=HIGH)

    b_adj = jnp.einsum("ln,hpn->hlp", bmat, g_in, precision=HIGH)
    c_state = jnp.einsum("ln,hpn->hlp", cmat, s_in, precision=HIGH)
    core = core_loc + leave[:, :, None] * b_adj
    gx = step_size[:, :, None] * core + skip_gain[:, None, None] * dys
    along = jnp.sum(xs * core, axis=2)
    from_state = enter * jnp.einsum(
        "hij,hi->hj", weights, jnp.sum(dys * c_state, axis=2), precision=HIGH
    )
    from_adj = leave * jnp.einsum(
        "hij,hj->hi", weights, jnp.sum(moved * b_adj, axis=2), precision=HIGH
    )
    both = leave * enter * jnp.sum(g_in * s_in, axis=(1, 2))[:, None]
    grad_step = along * (1.0 + rate * step_size) - rate * (inner + from_state + from_adj + both)
    gb = gb_loc + jnp.einsum("hlp,hpn->ln", left_u, g_in, precision=HIGH)
    gc = gc_loc + jnp.einsum("hlp,hpn->ln", enter_dy, s_in, precision=HIGH)

    grad_x = gx.transpose(1, 0, 2).reshape(length, heads * width)
    grad_bc = scatter_sum(jnp.stack([gb, gc]), "tensor")
    return (grad_x, grad_step, grad_bc[0], grad_bc[1])


def solution(mesh):
    in_specs = (
        P("context", "tensor"),
        P("context", "tensor"),
        P("tensor", "context"),
        P("tensor"),
        P("tensor"),
        P(("context", "tensor"), None),
        P(("context", "tensor"), None),
        P(),
    )
    out_specs = (
        P("context", "tensor"),
        P("tensor", "context"),
        P(("context", "tensor"), None),
        P(("context", "tensor"), None),
    )
    return jax.shard_map(local, mesh=mesh, in_specs=in_specs, out_specs=out_specs, check_vma=False)
```

```python
import jax
import jax.numpy as jnp
from jax import lax
from jax.sharding import PartitionSpec as P

HIGH = lax.Precision.HIGHEST


def from_behind(x, axis, by):
    peers = lax.axis_size(axis)
    pairs = [(i, i + by) for i in range(peers) if 0 <= i + by < peers]
    return lax.ppermute(x, axis, pairs)


FLOOR = -150.0


def pack(value, decay):
    top = jnp.max(jnp.abs(value), axis=-1, keepdims=True)
    expo = jnp.maximum(jnp.ceil(jnp.log2(jnp.where(top > 0, top, 1.0))), -100.0)
    code = jnp.clip(jnp.round(value / jnp.exp2(expo - 15.0)), -32767.0, 32767.0).astype(jnp.int16)
    scaled = decay * 64.0
    high = jnp.floor(scaled)
    low = jnp.round((scaled - high) * 16384.0)
    lanes = value.shape[-1]
    tail = jnp.concatenate([high, low, jnp.zeros((lanes - 2 * decay.shape[0],), jnp.float32)])[None]
    return jnp.concatenate(
        [code.reshape(-1, lanes), expo.reshape(-1, lanes).astype(jnp.int16), tail.astype(jnp.int16)]
    )


def unpack(packed, shape):
    body = shape[0] * shape[1]
    code = packed[:body].astype(jnp.float32).reshape(shape)
    expo = packed[body : body + body // shape[2]].astype(jnp.float32).reshape(shape[:2] + (1,))
    tail = packed[-1].astype(jnp.float32)
    decay = (tail[: shape[0]] + tail[shape[0] : 2 * shape[0]] / 16384.0) / 64.0
    return code * jnp.exp2(expo - 15.0), decay


def combine(own, got):
    value = own[0] + jnp.exp(own[1])[:, None, None] * got[0]
    return value, jnp.maximum(own[1] + got[1], FLOOR)


def shift_pair(fwd, bwd, by, held=()):
    shape = fwd[0].shape
    fwd, bwd, held = lax.optimization_barrier((pack(*fwd), pack(*bwd), held))
    got_f, got_b = from_behind(fwd, "context", by), from_behind(bwd, "context", -by)
    return unpack(got_f, shape), unpack(got_b, shape), held


def exchange(pieces, axis):
    count = lax.axis_size(axis)
    pieces = lax.optimization_barrier(pieces)
    got = [
        lax.ppermute(pieces[s], axis, [(i, (i + s) % count) for i in range(count)])
        for s in range(1, count)
    ]
    return [pieces[0]] + list(lax.optimization_barrier(got))


def scatter_sum(whole, axis):
    count = lax.axis_size(axis)
    size = whole.shape[1] // count
    parts = whole.reshape(whole.shape[0], count, size, whole.shape[2]).transpose(1, 0, 2, 3)
    got = lax.all_to_all(parts, axis, 0, 0, tiled=True)
    return jnp.sum(got, axis=0)


def scatter_sum_by_permutes(whole, axis):
    count = lax.axis_size(axis)
    me = lax.axis_index(axis)
    size = whole.shape[1] // count
    pieces = [
        lax.dynamic_slice_in_dim(whole, ((me + s) % count) * size, size, axis=1)
        for s in range(count)
    ]
    got = exchange(pieces, axis)
    out = got[0]
    for part in got[1:]:
        out = out + part
    return out


def local(inputs, grads, step_size, decay_rate, skip_gain, b_rows, c_rows, doc_lengths):
    length = inputs.shape[0]
    heads = step_size.shape[0]
    width = inputs.shape[1] // heads
    count = lax.axis_size("tensor")
    piece = jnp.stack([b_rows, c_rows])
    rows = lax.all_to_all(jnp.broadcast_to(piece, (count,) + piece.shape), "tensor", 0, 0, tiled=True)
    b_bf = rows[:, 0].reshape(length, -1)
    c_bf = rows[:, 1].reshape(length, -1)
    bmat = b_bf.astype(jnp.float32)
    cmat = c_bf.astype(jnp.float32)
    xs = inputs.astype(jnp.float32).reshape(length, heads, width).transpose(1, 0, 2)
    dys = grads.astype(jnp.float32).reshape(length, heads, width).transpose(1, 0, 2)
    offset = lax.axis_index("context") * length
    ends = jnp.cumsum(doc_lengths)
    starts = ends - doc_lengths
    position = offset + jnp.arange(length, dtype=jnp.int32)
    seg = jnp.sum(
        ((starts[None, :] >= offset) & (starts[None, :] <= position[:, None])).astype(jnp.int32),
        axis=1,
    )
    rate = decay_rate[:, None]
    logc = jnp.cumsum(-step_size * rate, axis=1)
    enter = jnp.exp(logc) * (seg == 0).astype(jnp.float32)[None, :]
    leave = jnp.exp(logc[:, -1:] - logc) * (seg == seg[-1]).astype(jnp.float32)[None, :]
    moved = step_size[:, :, None] * xs
    left_u = leave[:, :, None] * moved
    enter_dy = enter[:, :, None] * dys
    local_state = jnp.einsum("hlp,ln->hpn", left_u, bmat, precision=HIGH)
    local_adj = jnp.einsum("hlp,ln->hpn", enter_dy, cmat, precision=HIGH)

    reach = 3 * lax.axis_size("context") // 16
    low = reach & -reach
    high = reach - low
    assert high > 0 and high & (high - 1) == 0 and low < high
    shape = local_state.shape
    decay = jnp.where(seg[-1] == 0, jnp.maximum(logc[:, -1], FLOOR), FLOOR)
    fwd = (local_state, decay)
    bwd = (local_adj, decay)
    span = 1
    kept = {}
    held = (logc, dys, moved, b_bf, c_bf)
    while span < high:
        kept[span] = (fwd, bwd)
        if 2 * span < high:
            got_f, got_b, _ = shift_pair(fwd, bwd, span)
        else:
            got_f, got_b, held = shift_pair(fwd, bwd, span, held)
        fwd = combine(fwd, got_f)
        bwd = combine(bwd, got_b)
        span *= 2
    near_f, near_b = kept[low]
    sends = lax.optimization_barrier((pack(*near_f), pack(*fwd), pack(*near_b), pack(*bwd)))
    got = (
        from_behind(sends[0], "context", 1),
        from_behind(sends[1], "context", low + 1),
        from_behind(sends[2], "context", -1),
        from_behind(sends[3], "context", -low - 1),
    )
    got = [unpack(g, shape) for g in got]
    s_in = combine(got[0], got[1])[0]
    g_in = combine(got[2], got[3])[0]

    late_logc, late_dys, late_moved, late_b, late_c = held
    index = jnp.arange(length)
    keep = (index[:, None] >= index[None, :]) & (seg[:, None] == seg[None, :])
    weights = jnp.exp(
        jnp.where(keep[None], late_logc[:, :, None] - late_logc[:, None, :], -1e30)
    )
    scores = jnp.dot(late_c, late_b.T, preferred_element_type=jnp.float32)
    mixed = weights * scores[None]
    core_loc = jnp.einsum("hij,hip->hjp", mixed, late_dys, precision=HIGH)
    pairs = jnp.einsum("hip,hjp->hij", late_dys, late_moved, precision=HIGH)
    paired = mixed * pairs
    col_total = jnp.sum(paired, axis=1)
    row_total = jnp.sum(paired, axis=2)
    inner = jnp.cumsum(col_total, axis=1) - (jnp.cumsum(row_total, axis=1) - row_total)
    weighted = jnp.sum(weights * pairs, axis=0)
    gb_loc = jnp.dot(weighted.T, cmat, precision=HIGH)
    gc_loc = jnp.dot(weighted, bmat, precision=HIGH)

    b_adj = jnp.einsum("ln,hpn->hlp", bmat, g_in, precision=HIGH)
    c_state = jnp.einsum("ln,hpn->hlp", cmat, s_in, precision=HIGH)
    b_adj_t = jnp.einsum("ln,hpn->lhp", bmat, g_in, precision=HIGH)
    core_t = core_loc.transpose(1, 0, 2) + leave.T[:, :, None] * b_adj_t
    dys_t = grads.astype(jnp.float32).reshape(length, heads, width)
    xs_t = inputs.astype(jnp.float32).reshape(length, heads, width)
    gx_t = step_size.T[:, :, None] * core_t + skip_gain[None, :, None] * dys_t
    along = jnp.sum(xs_t * core_t, axis=2).T
    from_state = enter * jnp.einsum(
        "hij,hi->hj", weights, jnp.sum(dys * c_state, axis=2), precision=HIGH
    )
    from_adj = leave * jnp.einsum(
        "hij,hj->hi", weights, jnp.sum(moved * b_adj, axis=2), precision=HIGH
    )
    both = leave * enter * jnp.sum(g_in * s_in, axis=(1, 2))[:, None]
    grad_step = along * (1.0 + rate * step_size) - rate * (inner + from_state + from_adj + both)
    gb = gb_loc + jnp.einsum("hlp,hpn->ln", left_u, g_in, precision=HIGH)
    gc = gc_loc + jnp.einsum("hlp,hpn->ln", enter_dy, s_in, precision=HIGH)

    grad_x = gx_t.reshape(length, heads * width)
    grad_bc = scatter_sum(jnp.stack([gb, gc]), "tensor")
    return (grad_x, grad_step, grad_bc[0], grad_bc[1])


def solution(mesh):
    in_specs = (
        P("context", "tensor"),
        P("context", "tensor"),
        P("tensor", "context"),
        P("tensor"),
        P("tensor"),
        P(("context", "tensor"), None),
        P(("context", "tensor"), None),
        P(),
    )
    out_specs = (
        P("context", "tensor"),
        P("tensor", "context"),
        P(("context", "tensor"), None),
        P(("context", "tensor"), None),
    )
    return jax.shard_map(local, mesh=mesh, in_specs=in_specs, out_specs=out_specs, check_vma=False)
```

```python
import jax
import jax.numpy as jnp
from jax import lax
from jax.sharding import PartitionSpec as P

HIGH = lax.Precision.HIGHEST


def from_behind(x, axis, by):
    peers = lax.axis_size(axis)
    pairs = [(i, i + by) for i in range(peers) if 0 <= i + by < peers]
    return lax.ppermute(x, axis, pairs)


FLOOR = -150.0


def pack(value, decay):
    top = jnp.max(jnp.abs(value), axis=-1, keepdims=True)
    expo = jnp.maximum(jnp.ceil(jnp.log2(jnp.where(top > 0, top, 1.0))), -100.0)
    code = jnp.clip(jnp.round(value / jnp.exp2(expo - 15.0)), -32767.0, 32767.0).astype(jnp.int16)
    scaled = decay * 64.0
    high = jnp.floor(scaled)
    low = jnp.round((scaled - high) * 16384.0)
    lanes = value.shape[-1]
    tail = jnp.concatenate([high, low, jnp.zeros((lanes - 2 * decay.shape[0],), jnp.float32)])[None]
    return jnp.concatenate(
        [code.reshape(-1, lanes), expo.reshape(-1, lanes).astype(jnp.int16), tail.astype(jnp.int16)]
    )


def unpack(packed, shape):
    body = shape[0] * shape[1]
    code = packed[:body].astype(jnp.float32).reshape(shape)
    expo = packed[body : body + body // shape[2]].astype(jnp.float32).reshape(shape[:2] + (1,))
    tail = packed[-1].astype(jnp.float32)
    decay = (tail[: shape[0]] + tail[shape[0] : 2 * shape[0]] / 16384.0) / 64.0
    return code * jnp.exp2(expo - 15.0), decay


def combine(own, got):
    value = own[0] + jnp.exp(own[1])[:, None, None] * got[0]
    return value, jnp.maximum(own[1] + got[1], FLOOR)


def shift_pair(fwd, bwd, by, held=()):
    shape = fwd[0].shape
    fwd, bwd, held = lax.optimization_barrier((pack(*fwd), pack(*bwd), held))
    got_f, got_b = from_behind(fwd, "context", by), from_behind(bwd, "context", -by)
    return unpack(got_f, shape), unpack(got_b, shape), held


def exchange(pieces, axis):
    count = lax.axis_size(axis)
    pieces = lax.optimization_barrier(pieces)
    got = [
        lax.ppermute(pieces[s], axis, [(i, (i + s) % count) for i in range(count)])
        for s in range(1, count)
    ]
    return [pieces[0]] + list(lax.optimization_barrier(got))


def scatter_sum(whole, axis):
    count = lax.axis_size(axis)
    size = whole.shape[1] // count
    parts = whole.reshape(whole.shape[0], count, size, whole.shape[2]).transpose(1, 0, 2, 3)
    got = lax.all_to_all(parts, axis, 0, 0, tiled=True)
    return jnp.sum(got, axis=0)


def scatter_sum_by_permutes(whole, axis):
    count = lax.axis_size(axis)
    me = lax.axis_index(axis)
    size = whole.shape[1] // count
    pieces = [
        lax.dynamic_slice_in_dim(whole, ((me + s) % count) * size, size, axis=1)
        for s in range(count)
    ]
    got = exchange(pieces, axis)
    out = got[0]
    for part in got[1:]:
        out = out + part
    return out


def local(inputs, grads, step_size, decay_rate, skip_gain, b_rows, c_rows, doc_lengths):
    length = inputs.shape[0]
    heads = step_size.shape[0]
    width = inputs.shape[1] // heads
    count = lax.axis_size("tensor")
    piece = jnp.stack([b_rows, c_rows])
    rows = lax.all_to_all(jnp.broadcast_to(piece, (count,) + piece.shape), "tensor", 0, 0, tiled=True)
    b_bf = rows[:, 0].reshape(length, -1)
    c_bf = rows[:, 1].reshape(length, -1)
    bmat = b_bf.astype(jnp.float32)
    cmat = c_bf.astype(jnp.float32)
    xs = inputs.astype(jnp.float32).reshape(length, heads, width).transpose(1, 0, 2)
    dys = grads.astype(jnp.float32).reshape(length, heads, width).transpose(1, 0, 2)
    offset = lax.axis_index("context") * length
    ends = jnp.cumsum(doc_lengths)
    starts = ends - doc_lengths
    position = offset + jnp.arange(length, dtype=jnp.int32)
    seg = jnp.sum(
        ((starts[None, :] >= offset) & (starts[None, :] <= position[:, None])).astype(jnp.int32),
        axis=1,
    )
    rate = decay_rate[:, None]
    logc = jnp.cumsum(-step_size * rate, axis=1)
    enter = jnp.exp(logc) * (seg == 0).astype(jnp.float32)[None, :]
    leave = jnp.exp(logc[:, -1:] - logc) * (seg == seg[-1]).astype(jnp.float32)[None, :]
    moved = step_size[:, :, None] * xs
    left_u = leave[:, :, None] * moved
    enter_dy = enter[:, :, None] * dys
    local_state = jnp.einsum("hlp,ln->hpn", left_u, bmat, precision=lax.Precision.HIGH)
    local_adj = jnp.einsum("hlp,ln->hpn", enter_dy, cmat, precision=lax.Precision.HIGH)

    reach = 3 * lax.axis_size("context") // 16
    low = reach & -reach
    high = reach - low
    assert high > 0 and high & (high - 1) == 0 and low < high
    shape = local_state.shape
    decay = jnp.where(seg[-1] == 0, jnp.maximum(logc[:, -1], FLOOR), FLOOR)
    fwd = (local_state, decay)
    bwd = (local_adj, decay)
    span = 1
    kept = {}
    held = (logc, dys, moved, b_bf, c_bf)
    while span < high:
        kept[span] = (fwd, bwd)
        if 2 * span < high:
            got_f, got_b, _ = shift_pair(fwd, bwd, span)
        else:
            got_f, got_b, held = shift_pair(fwd, bwd, span, held)
        fwd = combine(fwd, got_f)
        bwd = combine(bwd, got_b)
        span *= 2
    near_f, near_b = kept[low]
    sends = lax.optimization_barrier((pack(*near_f), pack(*fwd), pack(*near_b), pack(*bwd)))
    got = (
        from_behind(sends[0], "context", 1),
        from_behind(sends[1], "context", low + 1),
        from_behind(sends[2], "context", -1),
        from_behind(sends[3], "context", -low - 1),
    )
    got = [unpack(g, shape) for g in got]
    s_in = combine(got[0], got[1])[0]
    g_in = combine(got[2], got[3])[0]

    late_logc, late_dys, late_moved, late_b, late_c = held
    index = jnp.arange(length)
    keep = (index[:, None] >= index[None, :]) & (seg[:, None] == seg[None, :])
    weights = jnp.exp(
        jnp.where(keep[None], late_logc[:, :, None] - late_logc[:, None, :], -1e30)
    )
    scores = jnp.dot(late_c, late_b.T, preferred_element_type=jnp.float32)
    mixed = weights * scores[None]
    core_loc = jnp.einsum("hij,hip->hjp", mixed, late_dys, precision=HIGH)
    pairs = jnp.einsum("hip,hjp->hij", late_dys, late_moved, precision=HIGH)
    paired = mixed * pairs
    col_total = jnp.sum(paired, axis=1)
    row_total = jnp.sum(paired, axis=2)
    inner = jnp.cumsum(col_total, axis=1) - (jnp.cumsum(row_total, axis=1) - row_total)
    weighted = jnp.sum(weights * pairs, axis=0)
    gb_loc = jnp.dot(weighted.T, cmat, precision=HIGH)
    gc_loc = jnp.dot(weighted, bmat, precision=HIGH)

    b_adj = jnp.einsum("ln,hpn->hlp", bmat, g_in, precision=HIGH)
    c_state = jnp.einsum("ln,hpn->hlp", cmat, s_in, precision=HIGH)
    core = core_loc + leave[:, :, None] * b_adj
    gx = step_size[:, :, None] * core + skip_gain[:, None, None] * dys
    along = jnp.sum(xs * core, axis=2)
    from_state = enter * jnp.einsum(
        "hij,hi->hj", weights, jnp.sum(dys * c_state, axis=2), precision=HIGH
    )
    from_adj = leave * jnp.einsum(
        "hij,hj->hi", weights, jnp.sum(moved * b_adj, axis=2), precision=HIGH
    )
    both = leave * enter * jnp.sum(g_in * s_in, axis=(1, 2))[:, None]
    grad_step = along * (1.0 + rate * step_size) - rate * (inner + from_state + from_adj + both)
    gb = gb_loc + jnp.einsum("hlp,hpn->ln", left_u, g_in, precision=HIGH)
    gc = gc_loc + jnp.einsum("hlp,hpn->ln", enter_dy, s_in, precision=HIGH)

    grad_x = gx.transpose(1, 0, 2).reshape(length, heads * width)
    grad_bc = scatter_sum(jnp.stack([gb, gc]), "tensor")
    return (grad_x, grad_step, grad_bc[0], grad_bc[1])


def solution(mesh):
    in_specs = (
        P("context", "tensor"),
        P("context", "tensor"),
        P("tensor", "context"),
        P("tensor"),
        P("tensor"),
        P(("context", "tensor"), None),
        P(("context", "tensor"), None),
        P(),
    )
    out_specs = (
        P("context", "tensor"),
        P("tensor", "context"),
        P(("context", "tensor"), None),
        P(("context", "tensor"), None),
    )
    return jax.shard_map(local, mesh=mesh, in_specs=in_specs, out_specs=out_specs, check_vma=False)
```

```python
import jax
import jax.numpy as jnp
from jax import lax
from jax.sharding import PartitionSpec as P

HIGH = lax.Precision.HIGHEST


def from_behind(x, axis, by):
    peers = lax.axis_size(axis)
    pairs = [(i, i + by) for i in range(peers) if 0 <= i + by < peers]
    return lax.ppermute(x, axis, pairs)


FLOOR = -150.0


def pack(value, decay):
    top = jnp.max(jnp.abs(value), axis=-1, keepdims=True)
    expo = jnp.maximum(jnp.ceil(jnp.log2(jnp.where(top > 0, top, 1.0))), -100.0)
    code = jnp.clip(jnp.round(value / jnp.exp2(expo - 15.0)), -32767.0, 32767.0).astype(jnp.int16)
    scaled = decay * 64.0
    high = jnp.floor(scaled)
    low = jnp.round((scaled - high) * 16384.0)
    lanes = value.shape[-1]
    tail = jnp.concatenate([high, low, jnp.zeros((lanes - 2 * decay.shape[0],), jnp.float32)])[None]
    return jnp.concatenate(
        [code.reshape(-1, lanes), expo.reshape(-1, lanes).astype(jnp.int16), tail.astype(jnp.int16)]
    )


def unpack(packed, shape):
    body = shape[0] * shape[1]
    code = packed[:body].astype(jnp.float32).reshape(shape)
    expo = packed[body : body + body // shape[2]].astype(jnp.float32).reshape(shape[:2] + (1,))
    tail = packed[-1].astype(jnp.float32)
    decay = (tail[: shape[0]] + tail[shape[0] : 2 * shape[0]] / 16384.0) / 64.0
    return code * jnp.exp2(expo - 15.0), decay


def combine(own, got):
    value = own[0] + jnp.exp(own[1])[:, None, None] * got[0]
    return value, jnp.maximum(own[1] + got[1], FLOOR)


def shift_pair(fwd, bwd, by, held=()):
    shape = fwd[0].shape
    fwd, bwd, held = lax.optimization_barrier((pack(*fwd), pack(*bwd), held))
    got_f, got_b = from_behind(fwd, "context", by), from_behind(bwd, "context", -by)
    return unpack(got_f, shape), unpack(got_b, shape), held


def exchange(pieces, axis):
    count = lax.axis_size(axis)
    pieces = lax.optimization_barrier(pieces)
    got = [
        lax.ppermute(pieces[s], axis, [(i, (i + s) % count) for i in range(count)])
        for s in range(1, count)
    ]
    return [pieces[0]] + list(lax.optimization_barrier(got))


def scatter_sum(whole, axis):
    count = lax.axis_size(axis)
    size = whole.shape[1] // count
    parts = whole.reshape(whole.shape[0], count, size, whole.shape[2]).transpose(1, 0, 2, 3)
    got = lax.all_to_all(parts, axis, 0, 0, tiled=True)
    return jnp.sum(got, axis=0)


def scatter_sum_by_permutes(whole, axis):
    count = lax.axis_size(axis)
    me = lax.axis_index(axis)
    size = whole.shape[1] // count
    pieces = [
        lax.dynamic_slice_in_dim(whole, ((me + s) % count) * size, size, axis=1)
        for s in range(count)
    ]
    got = exchange(pieces, axis)
    out = got[0]
    for part in got[1:]:
        out = out + part
    return out


def local(inputs, grads, step_size, decay_rate, skip_gain, b_rows, c_rows, doc_lengths):
    length = inputs.shape[0]
    heads = step_size.shape[0]
    width = inputs.shape[1] // heads
    count = lax.axis_size("tensor")
    piece = jnp.stack([b_rows, c_rows])
    rows = lax.all_to_all(jnp.broadcast_to(piece, (count,) + piece.shape), "tensor", 0, 0, tiled=True)
    b_bf = rows[:, 0].reshape(length, -1)
    c_bf = rows[:, 1].reshape(length, -1)
    bmat = b_bf.astype(jnp.float32)
    cmat = c_bf.astype(jnp.float32)
    xs = inputs.astype(jnp.float32).reshape(length, heads, width).transpose(1, 0, 2)
    dys = grads.astype(jnp.float32).reshape(length, heads, width).transpose(1, 0, 2)
    offset = lax.axis_index("context") * length
    ends = jnp.cumsum(doc_lengths)
    starts = ends - doc_lengths
    position = offset + jnp.arange(length, dtype=jnp.int32)
    seg = jnp.sum(
        ((starts[None, :] >= offset) & (starts[None, :] <= position[:, None])).astype(jnp.int32),
        axis=1,
    )
    rate = decay_rate[:, None]
    logc = jnp.cumsum(-step_size * rate, axis=1)
    enter = jnp.exp(logc) * (seg == 0).astype(jnp.float32)[None, :]
    leave = jnp.exp(logc[:, -1:] - logc) * (seg == seg[-1]).astype(jnp.float32)[None, :]
    moved = step_size[:, :, None] * xs
    left_u = leave[:, :, None] * moved
    enter_dy = enter[:, :, None] * dys
    local_state = jnp.einsum("hlp,ln->hpn", left_u, bmat, precision=lax.Precision.HIGH)
    local_adj = jnp.einsum("hlp,ln->hpn", enter_dy, cmat, precision=lax.Precision.HIGH)

    reach = 3 * lax.axis_size("context") // 16
    low = reach & -reach
    high = reach - low
    assert high > 0 and high & (high - 1) == 0 and low < high
    shape = local_state.shape
    decay = jnp.where(seg[-1] == 0, jnp.maximum(logc[:, -1], FLOOR), FLOOR)
    fwd = (local_state, decay)
    bwd = (local_adj, decay)
    span = 1
    kept = {}
    held = (logc, dys, moved, b_bf, c_bf)
    while span < high:
        kept[span] = (fwd, bwd)
        if 2 * span < high:
            got_f, got_b, _ = shift_pair(fwd, bwd, span)
        else:
            got_f, got_b, held = shift_pair(fwd, bwd, span, held)
        fwd = combine(fwd, got_f)
        bwd = combine(bwd, got_b)
        span *= 2
    near_f, near_b = kept[low]
    sends = lax.optimization_barrier((pack(*near_f), pack(*fwd), pack(*near_b), pack(*bwd)))
    got = (
        from_behind(sends[0], "context", 1),
        from_behind(sends[1], "context", low + 1),
        from_behind(sends[2], "context", -1),
        from_behind(sends[3], "context", -low - 1),
    )
    got = [unpack(g, shape) for g in got]
    s_in = combine(got[0], got[1])[0]
    g_in = combine(got[2], got[3])[0]

    late_logc, late_dys, late_moved, late_b, late_c = held
    index = jnp.arange(length)
    keep = (index[:, None] >= index[None, :]) & (seg[:, None] == seg[None, :])
    weights = jnp.exp(
        jnp.where(keep[None], late_logc[:, :, None] - late_logc[:, None, :], -1e30)
    )
    scores = jnp.dot(late_c, late_b.T, preferred_element_type=jnp.float32)
    mixed = weights * scores[None]
    core_loc = jnp.einsum("hij,hip->hjp", mixed, late_dys, precision=HIGH)
    pairs = jnp.einsum("hip,hjp->hij", late_dys, late_moved, precision=HIGH)
    paired = mixed * pairs
    col_total = jnp.sum(paired, axis=1)
    row_total = jnp.sum(paired, axis=2)
    inner = jnp.cumsum(col_total, axis=1) - (jnp.cumsum(row_total, axis=1) - row_total)
    weighted = jnp.sum(weights * pairs, axis=0)
    gb_loc = jnp.dot(weighted.T, cmat, precision=HIGH)
    gc_loc = jnp.dot(weighted, bmat, precision=HIGH)

    b_adj = jnp.einsum("ln,hpn->hlp", bmat, g_in, precision=lax.Precision.HIGH)
    c_state = jnp.einsum("ln,hpn->hlp", cmat, s_in, precision=lax.Precision.HIGH)
    core = core_loc + leave[:, :, None] * b_adj
    gx = step_size[:, :, None] * core + skip_gain[:, None, None] * dys
    along = jnp.sum(xs * core, axis=2)
    from_state = enter * jnp.einsum(
        "hij,hi->hj", weights, jnp.sum(dys * c_state, axis=2), precision=HIGH
    )
    from_adj = leave * jnp.einsum(
        "hij,hj->hi", weights, jnp.sum(moved * b_adj, axis=2), precision=HIGH
    )
    both = leave * enter * jnp.sum(g_in * s_in, axis=(1, 2))[:, None]
    grad_step = along * (1.0 + rate * step_size) - rate * (inner + from_state + from_adj + both)
    gb = gb_loc + jnp.einsum("hlp,hpn->ln", left_u, g_in, precision=HIGH)
    gc = gc_loc + jnp.einsum("hlp,hpn->ln", enter_dy, s_in, precision=HIGH)

    grad_x = gx.transpose(1, 0, 2).reshape(length, heads * width)
    grad_bc = scatter_sum(jnp.stack([gb, gc]), "tensor")
    return (grad_x, grad_step, grad_bc[0], grad_bc[1])


def solution(mesh):
    in_specs = (
        P("context", "tensor"),
        P("context", "tensor"),
        P("tensor", "context"),
        P("tensor"),
        P("tensor"),
        P(("context", "tensor"), None),
        P(("context", "tensor"), None),
        P(),
    )
    out_specs = (
        P("context", "tensor"),
        P("tensor", "context"),
        P(("context", "tensor"), None),
        P(("context", "tensor"), None),
    )
    return jax.shard_map(local, mesh=mesh, in_specs=in_specs, out_specs=out_specs, check_vma=False)
```
